256 devices in a mesh: chan: 64 (over z, x, y_lo), tm: 4 (over y_hi, core).
Axes of the slice: x: 4, y: 4 (y_hi: 2, y_lo: 2; y = y_hi * 2 + y_lo), z: 8, core: 2. Of those that a mesh axis runs over, the one named last changes fastest.
Arguments:
- raw_windows: bfloat16 [64, 4096, 2048], P('tm', 'chan'), may hold values from -480 to 480
- pairings: int32 [2, 64], replicated, may hold values from 0 to 63, as said below
Outputs:
- stacked_spectra: bfloat16 [2, 2, 4096, 64, 512], P(None, None, 'chan', None, 'tm')
The draws below stay inside these ranges and needn't reach their ends.
Inputs may be any that keep to these rules, and one draw needn't show every extreme that they name: Each row pairs the 64 blocks: pairings[r, pairings[r, b]] = b and no block is its own partner.
All inputs are finite; a program needn't handle non-finite values.
Results may differ from the reference program's by a relative error of at most 0.0075.
Values may be sent and summed in bfloat16 or wider, within the bound.
No kernel may reach another device: no remote copies, remote signals or barrier semaphores. Data moves between devices by JAX's collectives and lax.ppermute only.
A program may use at most 192 MiB of HBM per device.

```python
import math
import jax
import jax.numpy as jnp
from jax import lax

CB = 64
F = 512
L = 2048
W = 16
ROUNDS = 2
NBLOCKS = 64
CHANNELS = 4096
WINDOWS = 64
N_TM = 4


def draw_raw_windows(key, part):
    subkeys = jax.random.split(key, 5)
    full_shape = (WINDOWS, CHANNELS, L)
    noise_vals = jnp.clip(jax.random.normal(subkeys[0], full_shape, jnp.float32), -6.0, 6.0)
    top_scale = 10.0
    scales = jnp.exp(jax.random.uniform(subkeys[1], (WINDOWS, CHANNELS, 1), jnp.float32, 0.0, math.log(top_scale)))
    tone_amps = jax.random.uniform(subkeys[2], (WINDOWS, CHANNELS, 1), jnp.float32, 0.0, 24.0)
    tone_bins = jax.random.randint(subkeys[3], (WINDOWS, CHANNELS, 1), 1, F + 1)
    phases = jax.random.uniform(subkeys[4], (WINDOWS, CHANNELS, 1), jnp.float32, -math.pi, math.pi)
    samples = jnp.arange(L, dtype=jnp.int32)
    tone_turn = (tone_bins * samples % L).astype(jnp.float32) * (2.0 * math.pi / L)
    return (scales * (noise_vals + tone_amps * jnp.cos(tone_turn + phases))).astype(jnp.bfloat16)


def draw_pairings(key, part):

    def one_round(round_key):
        shuffled = jax.random.permutation(round_key, NBLOCKS).astype(jnp.int32)
        swapped = shuffled.reshape(NBLOCKS // 2, 2)[:, ::-1].reshape(NBLOCKS)
        return jnp.zeros((NBLOCKS,), jnp.int32).at[shuffled].set(swapped)
    return jax.vmap(one_round)(jax.random.split(jax.random.fold_in(key, 7), ROUNDS))


def setup_inputs(seed: int = 0) -> dict:
    key_list = jax.random.split(jax.random.key(seed), 3)
    raw_windows = draw_raw_windows(jax.random.fold_in(key_list[2], 71), 0)
    pairings = draw_pairings(jax.random.fold_in(key_list[2], 71), 0)
    return dict(raw_windows=raw_windows, pairings=pairings)


def make_table(freq_ids, imag_flag):
    samples = jnp.arange(L, dtype=jnp.int32)
    phase_ids = (freq_ids[:, None] + 1) * samples[None, :] % L
    angles = phase_ids.astype(jnp.float32) * (2.0 * math.pi / L)
    taper_vals = 0.5 - 0.5 * jnp.cos((samples.astype(jnp.float32) + 0.5) * (2.0 * math.pi / L))
    values = jnp.where(imag_flag[:, None] == 0, jnp.cos(angles), -jnp.sin(angles)) * taper_vals[None, :]
    return values.astype(jnp.bfloat16)

def product(left_arr, right_arr):
    return jnp.einsum('fdwa,fdwc->dacf', left_arr, right_arr, precision=lax.Precision.HIGHEST)

def reference(raw_windows, pairings):
    row_ids = jnp.arange(2 * F, dtype=jnp.int32)
    dft_table = make_table(row_ids % F, row_ids // F)

    def block_spectra(block_idx):
        block_raw = lax.dynamic_slice_in_dim(raw_windows, block_idx * CB, CB, 1)
        spectra = jnp.dot(dft_table, block_raw.reshape(WINDOWS * CB, L).T, preferred_element_type=jnp.float32)
        power_sum = lax.optimization_barrier(jnp.sum(spectra * spectra, axis=0)) / F
        whitened = (spectra / jnp.sqrt(power_sum + 1e-06)[None, :]).astype(jnp.bfloat16)
        return whitened.reshape(2, F, N_TM, W, CB)
    whitened_all = lax.map(block_spectra, jnp.arange(NBLOCKS, dtype=jnp.int32))
    scale_value = 1.0 / math.sqrt(WINDOWS)

    def block_stack(block_idx):
        own_spec = whitened_all[block_idx].astype(jnp.float32)
        outputs = []
        for round_idx in range(ROUNDS):
            partner = whitened_all[pairings[round_idx, block_idx]].astype(jnp.float32)
            real_sum = product(own_spec[0], partner[0]) + product(own_spec[1], partner[1])
            imag_sum = product(own_spec[1], partner[0]) - product(own_spec[0], partner[1])
            per_day = jnp.stack([real_sum, imag_sum], axis=1) * scale_value
            rounded = lax.optimization_barrier(per_day.astype(jnp.bfloat16)).astype(jnp.float32)
            outputs.append(lax.optimization_barrier(jnp.sum(rounded, axis=0)).astype(jnp.bfloat16))
        return jnp.stack(outputs)
    stacked = lax.map(block_stack, jnp.arange(NBLOCKS, dtype=jnp.int32))
    return jnp.transpose(stacked, (1, 2, 0, 3, 4, 5)).reshape(ROUNDS, 2, CHANNELS, CB, F)
```

```python
import math

import jax
import jax.numpy as jnp
from jax import lax
from jax.sharding import PartitionSpec as P

F = 512
L = 2048
ROUNDS = 2


def band_table(chan_count, day_count):
    per_piece = F // (chan_count * day_count)
    row_ids = jnp.arange(2 * F, dtype=jnp.int32)
    piece_idx = row_ids // (day_count * 2 * per_piece)
    remainder = row_ids % (day_count * 2 * per_piece)
    group_idx = remainder // (2 * per_piece)
    within = remainder % (2 * per_piece)
    imag_flag = within // per_piece
    offset_idx = within % per_piece
    freq_ids = group_idx * (chan_count * per_piece) + piece_idx * per_piece + offset_idx
    lanes = 128
    hi_ids = jnp.arange(L // lanes, dtype=jnp.int32)
    lo_ids = jnp.arange(lanes, dtype=jnp.int32)
    two_pi = 2.0 * math.pi / L
    hi_angle = ((freq_ids[:, None] + 1) * (hi_ids[None, :] * lanes) % L).astype(jnp.float32) * two_pi
    lo_angle = ((freq_ids[:, None] + 1) * lo_ids[None, :] % L).astype(jnp.float32) * two_pi
    hi_cos, hi_sin = jnp.cos(hi_angle), jnp.sin(hi_angle)
    lo_cos, lo_sin = jnp.cos(lo_angle), jnp.sin(lo_angle)
    is_real = (imag_flag == 0)[:, None]
    first = jnp.where(is_real, hi_cos, -hi_sin)
    second = jnp.where(is_real, -hi_sin, -hi_cos)
    samples = jnp.arange(L, dtype=jnp.int32).reshape(L // lanes, lanes)
    taper_vals = 0.5 - 0.5 * jnp.cos((samples.astype(jnp.float32) + 0.5) * (2.0 * math.pi / L))
    values = (
        first[:, :, None] * lo_cos[:, None, :] + second[:, :, None] * lo_sin[:, None, :]
    ) * taper_vals[None]
    values = values.reshape(2 * F, L)
    return values.astype(jnp.bfloat16)


def pair_tiles(spectra, partner_spec, scale_value):
    real_part = partner_spec[:, :, :, 0]
    imag_part = partner_spec[:, :, :, 1]
    rotated = jnp.stack([-imag_part, real_part], axis=3)
    both_terms = jnp.stack([partner_spec, rotated], axis=0)
    tile_vals = jnp.einsum(
        "bdtrjwa,qbdtrjwc->dtqacbj", spectra, both_terms, preferred_element_type=jnp.float32
    )
    return tile_vals * scale_value


def on_device(raw_windows, pairings):
    win_count, block_width, length = raw_windows.shape
    chan_count = lax.axis_size("chan")
    day_count = lax.axis_size("tm")
    per_piece = F // (chan_count * day_count)
    dft_table = band_table(chan_count, day_count)
    flat_raw = raw_windows.reshape(win_count * block_width, length)
    spectra = lax.dot_general(
        dft_table, flat_raw, (((1,), (1,)), ((), ())), preferred_element_type=jnp.float32
    )
    power_sum = jnp.sum(spectra * spectra, axis=0) / F
    whitened = (spectra * lax.rsqrt(power_sum + 1e-06)[None, :]).astype(jnp.bfloat16)
    layered = whitened.reshape(1, chan_count, day_count, 2 * per_piece, win_count * block_width)
    banded = lax.all_to_all(layered, "chan", split_axis=1, concat_axis=0, tiled=True)
    scale_value = 1.0 / math.sqrt(win_count * day_count)
    pooled = lax.all_to_all(banded, "tm", split_axis=2, concat_axis=1, tiled=True)
    banded_days = pooled.reshape(chan_count, day_count, 1, 2, per_piece, win_count, block_width)
    results = []
    for round_idx in range(ROUNDS):
        partner_spec = jnp.take(banded_days, pairings[round_idx], axis=0)
        tile_vals = pair_tiles(banded_days, partner_spec, scale_value)
        rounded = lax.optimization_barrier(tile_vals.astype(jnp.bfloat16)).astype(jnp.float32)
        summed = jnp.sum(rounded, axis=(0, 1))
        stacked = summed.reshape(2, block_width, block_width, chan_count * per_piece).astype(
            jnp.bfloat16
        )
        results.append(stacked)
    return lax.all_to_all(jnp.stack(results), "chan", split_axis=4, concat_axis=4, tiled=True)


def solution(mesh):
    return jax.shard_map(
        on_device,
        mesh=mesh,
        in_specs=(P("tm", "chan", None), P()),
        out_specs=P(None, None, "chan", None, "tm"),
        check_vma=False,
    )
```

```python
import functools
import math

import jax
import jax.numpy as jnp
from jax import lax
from jax.experimental import pallas as pl
from jax.experimental.pallas import tpu as pltpu
from jax.sharding import PartitionSpec as P

F = 512
L = 2048
ROUNDS = 2


def band_table(chan_count, day_count):
    per_piece = F // (chan_count * day_count)
    row_ids = jnp.arange(2 * F, dtype=jnp.int32)
    piece_idx = row_ids // (day_count * 2 * per_piece)
    remainder = row_ids % (day_count * 2 * per_piece)
    group_idx = remainder // (2 * per_piece)
    within = remainder % (2 * per_piece)
    imag_flag = within // per_piece
    offset_idx = within % per_piece
    freq_ids = group_idx * (chan_count * per_piece) + offset_idx * chan_count + piece_idx
    lanes = 128
    hi_ids = jnp.arange(L // lanes, dtype=jnp.int32)
    lo_ids = jnp.arange(lanes, dtype=jnp.int32)
    two_pi = 2.0 * math.pi / L
    hi_angle = ((freq_ids[:, None] + 1) * (hi_ids[None, :] * lanes) % L).astype(jnp.float32) * two_pi
    lo_angle = ((freq_ids[:, None] + 1) * lo_ids[None, :] % L).astype(jnp.float32) * two_pi
    hi_cos, hi_sin = jnp.cos(hi_angle), jnp.sin(hi_angle)
    lo_cos, lo_sin = jnp.cos(lo_angle), jnp.sin(lo_angle)
    is_real = (imag_flag == 0)[:, None]
    first = jnp.where(is_real, hi_cos, -hi_sin)
    second = jnp.where(is_real, -hi_sin, -hi_cos)
    samples = jnp.arange(L, dtype=jnp.int32).reshape(L // lanes, lanes)
    taper_vals = 0.5 - 0.5 * jnp.cos((samples.astype(jnp.float32) + 0.5) * (2.0 * math.pi / L))
    values = (
        first[:, :, None] * lo_cos[:, None, :] + second[:, :, None] * lo_sin[:, None, :]
    ) * taper_vals[None]
    values = values.reshape(2 * F, L)
    return values.astype(jnp.bfloat16)


def pair_kernel(pair_ref, x_ref, o_ref, *, group, day_count, half, width, scale_value):
    step = pl.program_id(0)
    round_idx = pl.program_id(1)
    lane = lax.broadcasted_iota(jnp.int32, (width, 2 * width), 1)
    low_lanes = lane < width

    def body(k, carry):
        block = step * group + k
        partner = pair_ref[round_idx, block]
        acc_re = jnp.zeros((width, 2 * width), jnp.float32)
        acc_im = jnp.zeros((width, 2 * width), jnp.float32)
        for day in range(day_count):
            own = x_ref[block, day]
            other = x_ref[partner, day]
            rotated = jnp.concatenate([-other[half:], other[:half]], axis=0)
            both = jnp.concatenate([other, rotated], axis=1)
            prods = [
                lax.dot_general(
                    own[:, off * width:(off + 1) * width], both,
                    (((0,), (0,)), ((), ())), preferred_element_type=jnp.float32,
                )
                for off in range(2)
            ]
            re = jnp.where(low_lanes, prods[0][:, :2 * width], prods[1][:, :2 * width])
            im = jnp.where(low_lanes, prods[0][:, 2 * width:], prods[1][:, 2 * width:])
            acc_re += (re * scale_value).astype(jnp.bfloat16).astype(jnp.float32)
            acc_im += (im * scale_value).astype(jnp.bfloat16).astype(jnp.float32)
        o_ref[k, 0, 0] = acc_re.astype(jnp.bfloat16)
        o_ref[k, 0, 1] = acc_im.astype(jnp.bfloat16)
        return carry

    lax.fori_loop(0, group, body, 0)


def pair_stage(pairings, spectra, scale_value):
    block_count, day_count, rows, lanes = spectra.shape
    width = lanes // 2
    group = 8
    kernel = functools.partial(
        pair_kernel, group=group, day_count=day_count, half=rows // 2, width=width,
        scale_value=scale_value,
    )
    return pl.pallas_call(
        kernel,
        grid_spec=pltpu.PrefetchScalarGridSpec(
            num_scalar_prefetch=1,
            grid=(block_count // group, ROUNDS),
            in_specs=[pl.BlockSpec(spectra.shape, lambda i, r, pr: (0, 0, 0, 0))],
            out_specs=pl.BlockSpec(
                (group, 1, 2, width, lanes), lambda i, r, pr: (i, r, 0, 0, 0)
            ),
        ),
        out_shape=jax.ShapeDtypeStruct((block_count, ROUNDS, 2, width, lanes), jnp.bfloat16),
    )(pairings, spectra)


def on_device(raw_windows, pairings):
    win_count, block_width, length = raw_windows.shape
    chan_count = lax.axis_size("chan")
    day_count = lax.axis_size("tm")
    per_piece = F // (chan_count * day_count)
    dft_table = band_table(chan_count, day_count)
    flat_raw = raw_windows.reshape(win_count * block_width, length)
    spectra = lax.dot_general(
        dft_table, flat_raw, (((1,), (1,)), ((), ())), preferred_element_type=jnp.float32
    )
    power_sum = jnp.sum(spectra * spectra, axis=0) / F
    whitened = (spectra * lax.rsqrt(power_sum + 1e-06)[None, :]).astype(jnp.bfloat16)
    layered = whitened.reshape(1, chan_count, day_count, 2 * per_piece, win_count * block_width)
    banded = lax.all_to_all(layered, "chan", split_axis=1, concat_axis=0, tiled=True)
    scale_value = 1.0 / math.sqrt(win_count * day_count)
    pooled = lax.all_to_all(banded, "tm", split_axis=2, concat_axis=1, tiled=True)
    by_block = pooled.reshape(chan_count, day_count, 2, per_piece, win_count, block_width)
    by_block = jnp.transpose(by_block, (0, 1, 2, 4, 3, 5)).reshape(
        chan_count, day_count, 2 * win_count, per_piece * block_width
    )
    tiles = pair_stage(pairings, by_block, scale_value)
    received = lax.all_to_all(tiles, "chan", split_axis=0, concat_axis=0, tiled=True)
    received = received.reshape(chan_count, ROUNDS, 2, block_width, per_piece, block_width)
    stacked = jnp.transpose(received, (1, 2, 3, 5, 4, 0))
    return stacked.reshape(ROUNDS, 2, block_width, block_width, per_piece * chan_count)


def solution(mesh):
    return jax.shard_map(
        on_device,
        mesh=mesh,
        in_specs=(P("tm", "chan", None), P()),
        out_specs=P(None, None, "chan", None, "tm"),
        check_vma=False,
    )
```

```python
import functools
import math

import jax
import jax.numpy as jnp
from jax import lax
from jax.experimental import pallas as pl
from jax.experimental.pallas import tpu as pltpu
from jax.sharding import PartitionSpec as P

F = 512
L = 2048
ROUNDS = 2


def band_table(chan_count, day_count):
    per_piece = F // (chan_count * day_count)
    row_ids = jnp.arange(2 * F, dtype=jnp.int32)
    piece_idx = row_ids // (day_count * 2 * per_piece)
    remainder = row_ids % (day_count * 2 * per_piece)
    group_idx = remainder // (2 * per_piece)
    within = remainder % (2 * per_piece)
    imag_flag = within // per_piece
    offset_idx = within % per_piece
    freq_ids = group_idx * (chan_count * per_piece) + offset_idx * chan_count + piece_idx
    lanes = 128
    hi_ids = jnp.arange(L // lanes, dtype=jnp.int32)
    lo_ids = jnp.arange(lanes, dtype=jnp.int32)
    two_pi = 2.0 * math.pi / L
    hi_angle = ((freq_ids[:, None] + 1) * (hi_ids[None, :] * lanes) % L).astype(jnp.float32) * two_pi
    lo_angle = ((freq_ids[:, None] + 1) * lo_ids[None, :] % L).astype(jnp.float32) * two_pi
    hi_cos, hi_sin = jnp.cos(hi_angle), jnp.sin(hi_angle)
    lo_cos, lo_sin = jnp.cos(lo_angle), jnp.sin(lo_angle)
    is_real = (imag_flag == 0)[:, None]
    first = jnp.where(is_real, hi_cos, -hi_sin)
    second = jnp.where(is_real, -hi_sin, -hi_cos)
    samples = jnp.arange(L, dtype=jnp.int32).reshape(L // lanes, lanes)
    taper_vals = 0.5 - 0.5 * jnp.cos((samples.astype(jnp.float32) + 0.5) * (2.0 * math.pi / L))
    values = (
        first[:, :, None] * lo_cos[:, None, :] + second[:, :, None] * lo_sin[:, None, :]
    ) * taper_vals[None]
    values = values.reshape(2 * F, L)
    return values.astype(jnp.bfloat16)


def pair_kernel(pair_ref, x_ref, o_ref, *, group, day_count, half, width, scale_value):
    step = pl.program_id(0)
    round_idx = pl.program_id(1)
    lane = lax.broadcasted_iota(jnp.int32, (width, 2 * width), 1)
    low_lanes = lane < width

    def body(k, carry):
        block = step * group + k
        partner = pair_ref[round_idx, block]
        acc_re = jnp.zeros((width, 2 * width), jnp.float32)
        acc_im = jnp.zeros((width, 2 * width), jnp.float32)
        for day in range(day_count):
            own = x_ref[block, day]
            other = x_ref[partner, day]
            rotated = jnp.concatenate([-other[half:], other[:half]], axis=0)
            both = jnp.concatenate([other, rotated], axis=1)
            prods = [
                lax.dot_general(
                    own[:, off * width:(off + 1) * width], both,
                    (((0,), (0,)), ((), ())), preferred_element_type=jnp.float32,
                )
                for off in range(2)
            ]
            re = jnp.where(low_lanes, prods[0][:, :2 * width], prods[1][:, :2 * width])
            im = jnp.where(low_lanes, prods[0][:, 2 * width:], prods[1][:, 2 * width:])
            acc_re += (re * scale_value).astype(jnp.bfloat16).astype(jnp.float32)
            acc_im += (im * scale_value).astype(jnp.bfloat16).astype(jnp.float32)
        o_ref[k, 0, 0] = acc_re.astype(jnp.bfloat16)
        o_ref[k, 0, 1] = acc_im.astype(jnp.bfloat16)
        return carry

    lax.fori_loop(0, group, body, 0)


def pair_stage(pairings, spectra, scale_value):
    block_count, day_count, rows, lanes = spectra.shape
    width = lanes // 2
    group = 8
    kernel = functools.partial(
        pair_kernel, group=group, day_count=day_count, half=rows // 2, width=width,
        scale_value=scale_value,
    )
    return pl.pallas_call(
        kernel,
        grid_spec=pltpu.PrefetchScalarGridSpec(
            num_scalar_prefetch=1,
            grid=(block_count // group, ROUNDS),
            in_specs=[pl.BlockSpec(spectra.shape, lambda i, r, pr: (0, 0, 0, 0))],
            out_specs=pl.BlockSpec(
                (group, 1, 2, width, lanes), lambda i, r, pr: (i, r, 0, 0, 0)
            ),
        ),
        out_shape=jax.ShapeDtypeStruct((block_count, ROUNDS, 2, width, lanes), jnp.bfloat16),
    )(pairings, spectra)


def unshuffle_kernel(x_ref, o_ref, *, group, width):
    for k in range(group):
        flipped = x_ref[k].astype(jnp.float32).T
        o_ref[k] = jnp.concatenate([flipped[:width], flipped[width:]], axis=1).astype(o_ref.dtype)


def unshuffle_stage(received):
    rows, sources, lanes = received.shape
    group = 16
    kernel = functools.partial(unshuffle_kernel, group=group, width=lanes // 2)
    return pl.pallas_call(
        kernel,
        grid=(rows // group,),
        in_specs=[pl.BlockSpec((group, sources, lanes), lambda i: (i, 0, 0))],
        out_specs=pl.BlockSpec((group, lanes // 2, 2 * sources), lambda i: (i, 0, 0)),
        out_shape=jax.ShapeDtypeStruct((rows, lanes // 2, 2 * sources), jnp.bfloat16),
    )(received)


def on_device(raw_windows, pairings):
    win_count, block_width, length = raw_windows.shape
    chan_count = lax.axis_size("chan")
    day_count = lax.axis_size("tm")
    per_piece = F // (chan_count * day_count)
    dft_table = band_table(chan_count, day_count)
    flat_raw = raw_windows.reshape(win_count * block_width, length)
    spectra = lax.dot_general(
        dft_table, flat_raw, (((1,), (1,)), ((), ())), preferred_element_type=jnp.float32
    )
    power_sum = jnp.sum(spectra * spectra, axis=0) / F
    whitened = (spectra * lax.rsqrt(power_sum + 1e-06)[None, :]).astype(jnp.bfloat16)
    layered = whitened.reshape(1, chan_count, day_count, 2 * per_piece, win_count * block_width)
    banded = lax.all_to_all(layered, "chan", split_axis=1, concat_axis=0, tiled=True)
    scale_value = 1.0 / math.sqrt(win_count * day_count)
    pooled = lax.all_to_all(banded, "tm", split_axis=2, concat_axis=1, tiled=True)
    by_block = pooled.reshape(chan_count, day_count, 2, per_piece, win_count, block_width)
    by_block = jnp.transpose(by_block, (0, 1, 2, 4, 3, 5)).reshape(
        chan_count, day_count, 2 * win_count, per_piece * block_width
    )
    tiles = pair_stage(pairings, by_block, scale_value)
    rows = ROUNDS * 2 * block_width
    tiles = tiles.reshape(chan_count, rows, 1, 2 * block_width)
    received = lax.all_to_all(tiles, "chan", split_axis=0, concat_axis=2, tiled=True)
    stacked = unshuffle_stage(received.reshape(rows, chan_count, 2 * block_width))
    return stacked.reshape(ROUNDS, 2, block_width, block_width, per_piece * chan_count)

def solution(mesh):
    return jax.shard_map(
        on_device,
        mesh=mesh,
        in_specs=(P("tm", "chan", None), P()),
        out_specs=P(None, None, "chan", None, "tm"),
        check_vma=False,
    )
```

```python
import functools
import math

import jax
import jax.numpy as jnp
from jax import lax
from jax.experimental import pallas as pl
from jax.experimental.pallas import tpu as pltpu
from jax.sharding import PartitionSpec as P

F = 512
L = 2048
ROUNDS = 2


def band_table(chan_count, day_count):
    per_piece = F // (chan_count * day_count)
    row_ids = jnp.arange(2 * F, dtype=jnp.int32)
    piece_idx = row_ids // (day_count * 2 * per_piece)
    remainder = row_ids % (day_count * 2 * per_piece)
    group_idx = remainder // (2 * per_piece)
    within = remainder % (2 * per_piece)
    imag_flag = within // per_piece
    offset_idx = within % per_piece
    freq_ids = group_idx * (chan_count * per_piece) + offset_idx * chan_count + piece_idx
    lanes = 128
    hi_ids = jnp.arange(L // lanes, dtype=jnp.int32)
    lo_ids = jnp.arange(lanes, dtype=jnp.int32)
    two_pi = 2.0 * math.pi / L
    hi_angle = ((freq_ids[:, None] + 1) * (hi_ids[None, :] * lanes) % L).astype(jnp.float32) * two_pi
    lo_angle = ((freq_ids[:, None] + 1) * lo_ids[None, :] % L).astype(jnp.float32) * two_pi
    hi_cos, hi_sin = jnp.cos(hi_angle), jnp.sin(hi_angle)
    lo_cos, lo_sin = jnp.cos(lo_angle), jnp.sin(lo_angle)
    is_real = (imag_flag == 0)[:, None]
    first = jnp.where(is_real, hi_cos, -hi_sin)
    second = jnp.where(is_real, -hi_sin, -hi_cos)
    samples = jnp.arange(L, dtype=jnp.int32).reshape(L // lanes, lanes)
    taper_vals = 0.5 - 0.5 * jnp.cos((samples.astype(jnp.float32) + 0.5) * (2.0 * math.pi / L))
    values = (
        first[:, :, None] * lo_cos[:, None, :] + second[:, :, None] * lo_sin[:, None, :]
    ) * taper_vals[None]
    values = values.reshape(2 * F, L)
    return values.astype(jnp.bfloat16)


def pair_kernel(pair_ref, x_ref, o_ref, *, group, day_count, half, width, scale_value):
    step = pl.program_id(0)
    rows = 2 * 2 * half
    row_part = lax.broadcasted_iota(jnp.int32, (rows, 2 * width), 0) // (2 * half)
    lane_part = lax.broadcasted_iota(jnp.int32, (rows, 2 * width), 1) // width
    diagonal = row_part == lane_part

    def spread(part):
        stacked = jnp.concatenate([part, part], axis=0)
        return jnp.where(diagonal, stacked, jnp.zeros_like(stacked))

    def body(k, carry):
        block = step * group + k
        partners = [pair_ref[r, block] for r in range(ROUNDS)]
        accs = [jnp.zeros((width, 4 * width), jnp.float32) for _ in range(ROUNDS)]
        for day in range(day_count):
            own = x_ref[block, day]
            lhs = jnp.concatenate([own[:, :width], own[:, width:]], axis=0)
            for r in range(ROUNDS):
                other = x_ref[partners[r], day]
                rotated = jnp.concatenate([-other[half:], other[:half]], axis=0)
                rhs = jnp.concatenate([spread(other), spread(rotated)], axis=1)
                prod = lax.dot_general(
                    lhs, rhs, (((0,), (0,)), ((), ())), preferred_element_type=jnp.float32
                )
                accs[r] = accs[r] + prod.astype(jnp.bfloat16).astype(jnp.float32)
        for r in range(ROUNDS):
            scaled = (accs[r] * scale_value).astype(jnp.bfloat16)
            o_ref[k, r, 0] = scaled[:, :2 * width]
            o_ref[k, r, 1] = scaled[:, 2 * width:]
        return carry

    lax.fori_loop(0, group, body, 0)


def pair_stage(pairings, spectra, scale_value):
    block_count, day_count, rows, lanes = spectra.shape
    width = lanes // 2
    group = 8
    kernel = functools.partial(
        pair_kernel, group=group, day_count=day_count, half=rows // 2, width=width,
        scale_value=scale_value,
    )
    return pl.pallas_call(
        kernel,
        grid_spec=pltpu.PrefetchScalarGridSpec(
            num_scalar_prefetch=1,
            grid=(block_count // group,),
            in_specs=[pl.BlockSpec(spectra.shape, lambda i, pr: (0, 0, 0, 0))],
            out_specs=pl.BlockSpec(
                (group, ROUNDS, 2, width, lanes), lambda i, pr: (i, 0, 0, 0, 0)
            ),
        ),
        out_shape=jax.ShapeDtypeStruct((block_count, ROUNDS, 2, width, lanes), jnp.bfloat16),
    )(pairings, spectra)

def unshuffle_kernel(x_ref, o_ref, *, group, width):
    for k in range(group):
        flipped = x_ref[k].astype(jnp.float32).T
        o_ref[k] = jnp.concatenate([flipped[:width], flipped[width:]], axis=1).astype(o_ref.dtype)


def unshuffle_stage(received):
    rows, sources, lanes = received.shape
    group = 16
    kernel = functools.partial(unshuffle_kernel, group=group, width=lanes // 2)
    return pl.pallas_call(
        kernel,
        grid=(rows // group,),
        in_specs=[pl.BlockSpec((group, sources, lanes), lambda i: (i, 0, 0))],
        out_specs=pl.BlockSpec((group, lanes // 2, 2 * sources), lambda i: (i, 0, 0)),
        out_shape=jax.ShapeDtypeStruct((rows, lanes // 2, 2 * sources), jnp.bfloat16),
    )(received)


def on_device(raw_windows, pairings):
    win_count, block_width, length = raw_windows.shape
    chan_count = lax.axis_size("chan")
    day_count = lax.axis_size("tm")
    per_piece = F // (chan_count * day_count)
    dft_table = band_table(chan_count, day_count)
    flat_raw = raw_windows.reshape(win_count * block_width, length)
    spectra = lax.dot_general(
        dft_table, flat_raw, (((1,), (1,)), ((), ())), preferred_element_type=jnp.float32
    )
    power_sum = jnp.sum(spectra * spectra, axis=0) / F
    whitened = (spectra * lax.rsqrt(power_sum + 1e-06)[None, :]).astype(jnp.bfloat16)
    layered = whitened.reshape(1, chan_count, day_count, 2 * per_piece, win_count * block_width)
    banded = lax.all_to_all(layered, "chan", split_axis=1, concat_axis=0, tiled=True)
    scale_value = 1.0 / math.sqrt(win_count * day_count)
    pooled = lax.all_to_all(banded, "tm", split_axis=2, concat_axis=1, tiled=True)
    by_block = pooled.reshape(chan_count, day_count, 2, per_piece, win_count, block_width)
    by_block = jnp.transpose(by_block, (0, 1, 2, 4, 3, 5)).reshape(
        chan_count, day_count, 2 * win_count, per_piece * block_width
    )
    tiles = pair_stage(pairings, by_block, scale_value)
    rows = ROUNDS * 2 * block_width
    tiles = tiles.reshape(chan_count, rows, 1, 2 * block_width)
    received = lax.all_to_all(tiles, "chan", split_axis=0, concat_axis=2, tiled=True)
    stacked = unshuffle_stage(received.reshape(rows, chan_count, 2 * block_width))
    return stacked.reshape(ROUNDS, 2, block_width, block_width, per_piece * chan_count)

def solution(mesh):
    return jax.shard_map(
        on_device,
        mesh=mesh,
        in_specs=(P("tm", "chan", None), P()),
        out_specs=P(None, None, "chan", None, "tm"),
        check_vma=False,
    )
```

```python
import functools
import math

import jax
import jax.numpy as jnp
from jax import lax
from jax.experimental import pallas as pl
from jax.experimental.pallas import tpu as pltpu
from jax.sharding import PartitionSpec as P

F = 512
L = 2048
ROUNDS = 2


def band_table(chan_count, day_count):
    per_piece = F // (chan_count * day_count)
    row_ids = jnp.arange(2 * F, dtype=jnp.int32)
    piece_idx = row_ids // (day_count * 2 * per_piece)
    remainder = row_ids % (day_count * 2 * per_piece)
    group_idx = remainder // (2 * per_piece)
    within = remainder % (2 * per_piece)
    imag_flag = within // per_piece
    offset_idx = within % per_piece
    freq_ids = group_idx * (chan_count * per_piece) + offset_idx * chan_count + piece_idx
    lanes = 128
    hi_ids = jnp.arange(L // lanes, dtype=jnp.int32)
    lo_ids = jnp.arange(lanes, dtype=jnp.int32)
    two_pi = 2.0 * math.pi / L
    hi_angle = ((freq_ids[:, None] + 1) * (hi_ids[None, :] * lanes) % L).astype(jnp.float32) * two_pi
    lo_angle = ((freq_ids[:, None] + 1) * lo_ids[None, :] % L).astype(jnp.float32) * two_pi
    hi_cos, hi_sin = jnp.cos(hi_angle), jnp.sin(hi_angle)
    lo_cos, lo_sin = jnp.cos(lo_angle), jnp.sin(lo_angle)
    is_real = (imag_flag == 0)[:, None]
    first = jnp.where(is_real, hi_cos, -hi_sin)
    second = jnp.where(is_real, -hi_sin, -hi_cos)
    samples = jnp.arange(L, dtype=jnp.int32).reshape(L // lanes, lanes)
    taper_vals = 0.5 - 0.5 * jnp.cos((samples.astype(jnp.float32) + 0.5) * (2.0 * math.pi / L))
    values = (
        first[:, :, None] * lo_cos[:, None, :] + second[:, :, None] * lo_sin[:, None, :]
    ) * taper_vals[None]
    values = values.reshape(2 * F, L)
    return values.astype(jnp.bfloat16)


def pair_kernel(pair_ref, x_ref, o_ref, *, group, day_count, half, width, scale_value):
    step = pl.program_id(0)
    rows = 2 * 2 * half
    row_part = lax.broadcasted_iota(jnp.int32, (rows, 2 * width), 0) // (2 * half)
    lane_part = lax.broadcasted_iota(jnp.int32, (rows, 2 * width), 1) // width
    diagonal = row_part == lane_part

    def spread(part):
        stacked = jnp.concatenate([part, part], axis=0)
        return jnp.where(diagonal, stacked, jnp.zeros_like(stacked))

    def body(k, carry):
        block = step * group + k
        partners = [pair_ref[r, block] for r in range(ROUNDS)]
        accs = [jnp.zeros((width, 4 * width), jnp.float32) for _ in range(ROUNDS)]
        for day in range(day_count):
            own = x_ref[block, day]
            lhs = jnp.concatenate([own[:, :width], own[:, width:]], axis=0)
            for r in range(ROUNDS):
                other = x_ref[partners[r], day]
                rotated = jnp.concatenate([-other[half:], other[:half]], axis=0)
                rhs = jnp.concatenate([spread(other), spread(rotated)], axis=1)
                prod = lax.dot_general(
                    lhs, rhs, (((0,), (0,)), ((), ())), preferred_element_type=jnp.float32
                )
                accs[r] = accs[r] + prod.astype(jnp.bfloat16).astype(jnp.float32)
        for r in range(ROUNDS):
            scaled = (accs[r] * scale_value).astype(jnp.bfloat16)
            o_ref[k, r, 0] = scaled[:, :2 * width]
            o_ref[k, r, 1] = scaled[:, 2 * width:]
        return carry

    lax.fori_loop(0, group, body, 0)


def pair_stage(pairings, spectra, scale_value):
    block_count, day_count, rows, lanes = spectra.shape
    width = lanes // 2
    group = 8
    kernel = functools.partial(
        pair_kernel, group=group, day_count=day_count, half=rows // 2, width=width,
        scale_value=scale_value,
    )
    return pl.pallas_call(
        kernel,
        grid_spec=pltpu.PrefetchScalarGridSpec(
            num_scalar_prefetch=1,
            grid=(block_count // group,),
            in_specs=[pl.BlockSpec(spectra.shape, lambda i, pr: (0, 0, 0, 0))],
            out_specs=pl.BlockSpec(
                (group, ROUNDS, 2, width, lanes), lambda i, pr: (i, 0, 0, 0, 0)
            ),
        ),
        out_shape=jax.ShapeDtypeStruct((block_count, ROUNDS, 2, width, lanes), jnp.bfloat16),
    )(pairings, spectra)

def unshuffle_kernel(x_ref, o_ref, *, group, width):
    for k in range(group):
        flipped = x_ref[k].astype(jnp.float32).T
        o_ref[k] = jnp.concatenate([flipped[:width], flipped[width:]], axis=1).astype(o_ref.dtype)


def unshuffle_stage(received):
    rows, sources, lanes = received.shape
    group = 16
    kernel = functools.partial(unshuffle_kernel, group=group, width=lanes // 2)
    return pl.pallas_call(
        kernel,
        grid=(rows // group,),
        in_specs=[pl.BlockSpec((group, sources, lanes), lambda i: (i, 0, 0))],
        out_specs=pl.BlockSpec((group, lanes // 2, 2 * sources), lambda i: (i, 0, 0)),
        out_shape=jax.ShapeDtypeStruct((rows, lanes // 2, 2 * sources), jnp.bfloat16),
    )(received)


def on_device(raw_windows, pairings):
    win_count, block_width, length = raw_windows.shape
    chan_count = lax.axis_size("chan")
    day_count = lax.axis_size("tm")
    per_piece = F // (chan_count * day_count)
    dft_table = band_table(chan_count, day_count)
    flat_raw = raw_windows.reshape(win_count * block_width, length)
    spectra = lax.dot_general(
        dft_table, flat_raw, (((1,), (1,)), ((), ())), preferred_element_type=jnp.float32
    )
    power_sum = jnp.sum(spectra * spectra, axis=0) / F
    whitened = (spectra * lax.rsqrt(power_sum + 1e-06)[None, :]).astype(jnp.bfloat16)
    layered = whitened.reshape(chan_count * day_count, 2 * per_piece, win_count * block_width)
    scale_value = 1.0 / math.sqrt(win_count * day_count)
    pooled = lax.all_to_all(layered, ("chan", "tm"), split_axis=0, concat_axis=0, tiled=True)
    by_block = pooled.reshape(chan_count, day_count, 2, per_piece, win_count, block_width)
    by_block = jnp.transpose(by_block, (0, 1, 2, 4, 3, 5)).reshape(
        chan_count, day_count, 2 * win_count, per_piece * block_width
    )
    tiles = pair_stage(pairings, by_block, scale_value)
    rows = ROUNDS * 2 * block_width
    tiles = tiles.reshape(chan_count, rows, 1, 2 * block_width)
    received = lax.all_to_all(tiles, "chan", split_axis=0, concat_axis=2, tiled=True)
    stacked = unshuffle_stage(received.reshape(rows, chan_count, 2 * block_width))
    return stacked.reshape(ROUNDS, 2, block_width, block_width, per_piece * chan_count)

def solution(mesh):
    return jax.shard_map(
        on_device,
        mesh=mesh,
        in_specs=(P("tm", "chan", None), P()),
        out_specs=P(None, None, "chan", None, "tm"),
        check_vma=False,
    )
```

```python
import functools
import math

import jax
import jax.numpy as jnp
from jax import lax
from jax.experimental import pallas as pl
from jax.experimental.pallas import tpu as pltpu
from jax.sharding import PartitionSpec as P

F = 512
L = 2048
ROUNDS = 2


def band_table(chan_count, day_count):
    per_piece = F // (chan_count * day_count)
    row_ids = jnp.arange(2 * F, dtype=jnp.int32)
    piece_idx = row_ids // (day_count * 2 * per_piece)
    remainder = row_ids % (day_count * 2 * per_piece)
    group_idx = remainder // (2 * per_piece)
    within = remainder % (2 * per_piece)
    imag_flag = within // per_piece
    offset_idx = within % per_piece
    freq_ids = group_idx * (chan_count * per_piece) + offset_idx * chan_count + piece_idx
    lanes = 128
    hi_ids = jnp.arange(L // lanes, dtype=jnp.int32)
    lo_ids = jnp.arange(lanes, dtype=jnp.int32)
    two_pi = 2.0 * math.pi / L
    hi_angle = ((freq_ids[:, None] + 1) * (hi_ids[None, :] * lanes) % L).astype(jnp.float32) * two_pi
    lo_angle = ((freq_ids[:, None] + 1) * lo_ids[None, :] % L).astype(jnp.float32) * two_pi
    hi_cos, hi_sin = jnp.cos(hi_angle), jnp.sin(hi_angle)
    lo_cos, lo_sin = jnp.cos(lo_angle), jnp.sin(lo_angle)
    is_real = (imag_flag == 0)[:, None]
    first = jnp.where(is_real, hi_cos, -hi_sin)
    second = jnp.where(is_real, -hi_sin, -hi_cos)
    samples = jnp.arange(L, dtype=jnp.int32).reshape(L // lanes, lanes)
    taper_vals = 0.5 - 0.5 * jnp.cos((samples.astype(jnp.float32) + 0.5) * (2.0 * math.pi / L))
    values = (
        first[:, :, None] * lo_cos[:, None, :] + second[:, :, None] * lo_sin[:, None, :]
    ) * taper_vals[None]
    values = values.reshape(2 * F, L)
    return values.astype(jnp.bfloat16)


def pair_kernel(pair_ref, x_ref, o_ref, *, group, day_count, half, width, scale_value, rounds):
    step = pl.program_id(0)
    rows = 2 * 2 * half
    row_part = lax.broadcasted_iota(jnp.int32, (rows, 2 * width), 0) // (2 * half)
    lane_part = lax.broadcasted_iota(jnp.int32, (rows, 2 * width), 1) // width
    diagonal = row_part == lane_part

    def spread(part):
        stacked = jnp.concatenate([part, part], axis=0)
        return jnp.where(diagonal, stacked, jnp.zeros_like(stacked))

    def body(k, carry):
        block = step * group + k
        partners = [pair_ref[r, block] for r in rounds]
        accs = [jnp.zeros((width, 4 * width), jnp.float32) for _ in rounds]
        for day in range(day_count):
            own = x_ref[block, day]
            lhs = jnp.concatenate([own[:, :width], own[:, width:]], axis=0)
            for r in range(len(rounds)):
                other = x_ref[partners[r], day]
                rotated = jnp.concatenate([-other[half:], other[:half]], axis=0)
                rhs = jnp.concatenate([spread(other), spread(rotated)], axis=1)
                prod = lax.dot_general(
                    lhs, rhs, (((0,), (0,)), ((), ())), preferred_element_type=jnp.float32
                )
                accs[r] = accs[r] + prod.astype(jnp.bfloat16).astype(jnp.float32)
        for r in range(len(rounds)):
            scaled = (accs[r] * scale_value).astype(jnp.bfloat16)
            o_ref[k, r, 0] = scaled[:, :2 * width]
            o_ref[k, r, 1] = scaled[:, 2 * width:]
        return carry

    lax.fori_loop(0, group, body, 0)


def pair_stage(pairings, spectra, scale_value, rounds=tuple(range(ROUNDS))):
    block_count, day_count, rows, lanes = spectra.shape
    width = lanes // 2
    group = 8
    kernel = functools.partial(
        pair_kernel, group=group, day_count=day_count, half=rows // 2, width=width,
        scale_value=scale_value, rounds=rounds,
    )
    return pl.pallas_call(
        kernel,
        grid_spec=pltpu.PrefetchScalarGridSpec(
            num_scalar_prefetch=1,
            grid=(block_count // group,),
            in_specs=[pl.BlockSpec(spectra.shape, lambda i, pr: (0, 0, 0, 0))],
            out_specs=pl.BlockSpec(
                (group, len(rounds), 2, width, lanes), lambda i, pr: (i, 0, 0, 0, 0)
            ),
        ),
        out_shape=jax.ShapeDtypeStruct((block_count, len(rounds), 2, width, lanes), jnp.bfloat16),
    )(pairings, spectra)

def unshuffle_kernel(x_ref, o_ref, *, group, width):
    for k in range(group):
        flipped = x_ref[k].astype(jnp.float32).T
        o_ref[k] = jnp.concatenate([flipped[:width], flipped[width:]], axis=1).astype(o_ref.dtype)


def unshuffle_stage(received):
    rows, sources, lanes = received.shape
    group = 16
    kernel = functools.partial(unshuffle_kernel, group=group, width=lanes // 2)
    return pl.pallas_call(
        kernel,
        grid=(rows // group,),
        in_specs=[pl.BlockSpec((group, sources, lanes), lambda i: (i, 0, 0))],
        out_specs=pl.BlockSpec((group, lanes // 2, 2 * sources), lambda i: (i, 0, 0)),
        out_shape=jax.ShapeDtypeStruct((rows, lanes // 2, 2 * sources), jnp.bfloat16),
    )(received)


def on_device(raw_windows, pairings):
    win_count, block_width, length = raw_windows.shape
    chan_count = lax.axis_size("chan")
    day_count = lax.axis_size("tm")
    per_piece = F // (chan_count * day_count)
    dft_table = band_table(chan_count, day_count)
    flat_raw = raw_windows.reshape(win_count * block_width, length)
    spectra = lax.dot_general(
        dft_table, flat_raw, (((1,), (1,)), ((), ())), preferred_element_type=jnp.float32
    )
    power_sum = jnp.sum(spectra * spectra, axis=0) / F
    whitened = (spectra * lax.rsqrt(power_sum + 1e-06)[None, :]).astype(jnp.bfloat16)
    layered = whitened.reshape(chan_count * day_count, 2 * per_piece, win_count * block_width)
    scale_value = 1.0 / math.sqrt(win_count * day_count)
    pooled = lax.all_to_all(layered, ("chan", "tm"), split_axis=0, concat_axis=0, tiled=True)
    by_block = pooled.reshape(chan_count, day_count, 2, per_piece, win_count, block_width)
    by_block = jnp.transpose(by_block, (0, 1, 2, 4, 3, 5)).reshape(
        chan_count, day_count, 2 * win_count, per_piece * block_width
    )
    rows = 2 * block_width
    parts = []
    for round_idx in range(ROUNDS):
        tiles = pair_stage(pairings, by_block, scale_value, (round_idx,))
        tiles = tiles.reshape(chan_count, rows, 1, 2 * block_width)
        received = lax.all_to_all(tiles, "chan", split_axis=0, concat_axis=2, tiled=True)
        parts.append(unshuffle_stage(received.reshape(rows, chan_count, 2 * block_width)))
    stacked = jnp.stack(parts)
    return stacked.reshape(ROUNDS, 2, block_width, block_width, per_piece * chan_count)

def solution(mesh):
    return jax.shard_map(
        on_device,
        mesh=mesh,
        in_specs=(P("tm", "chan", None), P()),
        out_specs=P(None, None, "chan", None, "tm"),
        check_vma=False,
    )
```

```python
import functools
import math

import jax
import ml_dtypes
import numpy as np
import jax.numpy as jnp
from jax import lax
from jax.experimental import pallas as pl
from jax.experimental.pallas import tpu as pltpu
from jax.sharding import PartitionSpec as P

F = 512
L = 2048
ROUNDS = 2


def band_table(chan_count, day_count):
    per_piece = F // (chan_count * day_count)
    row_ids = np.arange(2 * F, dtype=np.int64)
    piece_idx = row_ids // (day_count * 2 * per_piece)
    remainder = row_ids % (day_count * 2 * per_piece)
    group_idx = remainder // (2 * per_piece)
    within = remainder % (2 * per_piece)
    imag_flag = within // per_piece
    offset_idx = within % per_piece
    freq_ids = group_idx * (chan_count * per_piece) + offset_idx * chan_count + piece_idx
    samples = np.arange(L, dtype=np.int64)
    angles = ((freq_ids[:, None] + 1) * samples[None, :] % L) * (2.0 * np.pi / L)
    taper_vals = 0.5 - 0.5 * np.cos((samples + 0.5) * (2.0 * np.pi / L))
    values = np.where(imag_flag[:, None] == 0, np.cos(angles), -np.sin(angles)) * taper_vals[None]
    return jnp.asarray(values.astype(ml_dtypes.bfloat16))

def pair_kernel(pair_ref, x_ref, o_ref, *, group, day_count, half, width, scale_value):
    step = pl.program_id(0)
    rows = 2 * 2 * half
    row_part = lax.broadcasted_iota(jnp.int32, (rows, 2 * width), 0) // (2 * half)
    lane_part = lax.broadcasted_iota(jnp.int32, (rows, 2 * width), 1) // width
    diagonal = row_part == lane_part

    def spread(part):
        stacked = jnp.concatenate([part, part], axis=0)
        return jnp.where(diagonal, stacked, jnp.zeros_like(stacked))

    def body(k, carry):
        block = step * group + k
        partners = [pair_ref[r, block] for r in range(ROUNDS)]
        accs = [jnp.zeros((width, 4 * width), jnp.float32) for _ in range(ROUNDS)]
        for day in range(day_count):
            own = x_ref[block, day]
            lhs = jnp.concatenate([own[:, :width], own[:, width:]], axis=0)
            for r in range(ROUNDS):
                other = x_ref[partners[r], day]
                rotated = jnp.concatenate([-other[half:], other[:half]], axis=0)
                rhs = jnp.concatenate([spread(other), spread(rotated)], axis=1)
                prod = lax.dot_general(
                    lhs, rhs, (((0,), (0,)), ((), ())), preferred_element_type=jnp.float32
                )
                accs[r] = accs[r] + prod.astype(jnp.bfloat16).astype(jnp.float32)
        for r in range(ROUNDS):
            scaled = (accs[r] * scale_value).astype(jnp.bfloat16)
            o_ref[k, r, 0] = scaled[:, :2 * width]
            o_ref[k, r, 1] = scaled[:, 2 * width:]
        return carry

    lax.fori_loop(0, group, body, 0)


def pair_stage(pairings, spectra, scale_value):
    block_count, day_count, rows, lanes = spectra.shape
    width = lanes // 2
    group = 8
    kernel = functools.partial(
        pair_kernel, group=group, day_count=day_count, half=rows // 2, width=width,
        scale_value=scale_value,
    )
    return pl.pallas_call(
        kernel,
        grid_spec=pltpu.PrefetchScalarGridSpec(
            num_scalar_prefetch=1,
            grid=(block_count // group,),
            in_specs=[pl.BlockSpec(spectra.shape, lambda i, pr: (0, 0, 0, 0))],
            out_specs=pl.BlockSpec(
                (group, ROUNDS, 2, width, lanes), lambda i, pr: (i, 0, 0, 0, 0)
            ),
        ),
        out_shape=jax.ShapeDtypeStruct((block_count, ROUNDS, 2, width, lanes), jnp.bfloat16),
    )(pairings, spectra)

def unshuffle_kernel(x_ref, o_ref, *, group, width):
    for k in range(group):
        flipped = x_ref[k].astype(jnp.float32).T
        o_ref[k] = jnp.concatenate([flipped[:width], flipped[width:]], axis=1).astype(o_ref.dtype)


def unshuffle_stage(received):
    rows, sources, lanes = received.shape
    group = 16
    kernel = functools.partial(unshuffle_kernel, group=group, width=lanes // 2)
    return pl.pallas_call(
        kernel,
        grid=(rows // group,),
        in_specs=[pl.BlockSpec((group, sources, lanes), lambda i: (i, 0, 0))],
        out_specs=pl.BlockSpec((group, lanes // 2, 2 * sources), lambda i: (i, 0, 0)),
        out_shape=jax.ShapeDtypeStruct((rows, lanes // 2, 2 * sources), jnp.bfloat16),
    )(received)


def on_device(raw_windows, pairings):
    win_count, block_width, length = raw_windows.shape
    chan_count = lax.axis_size("chan")
    day_count = lax.axis_size("tm")
    per_piece = F // (chan_count * day_count)
    dft_table = band_table(chan_count, day_count)
    flat_raw = raw_windows.reshape(win_count * block_width, length)
    spectra = lax.dot_general(
        dft_table, flat_raw, (((1,), (1,)), ((), ())), preferred_element_type=jnp.float32
    )
    power_sum = jnp.sum(spectra * spectra, axis=0) / F
    whitened = (spectra * lax.rsqrt(power_sum + 1e-06)[None, :]).astype(jnp.bfloat16)
    layered = whitened.reshape(chan_count * day_count, 2 * per_piece, win_count * block_width)
    scale_value = 1.0 / math.sqrt(win_count * day_count)
    pooled = lax.all_to_all(layered, ("chan", "tm"), split_axis=0, concat_axis=0, tiled=True)
    by_block = pooled.reshape(chan_count, day_count, 2, per_piece, win_count, block_width)
    by_block = jnp.transpose(by_block, (0, 1, 2, 4, 3, 5)).reshape(
        chan_count, day_count, 2 * win_count, per_piece * block_width
    )
    tiles = pair_stage(pairings, by_block, scale_value)
    rows = ROUNDS * 2 * block_width
    tiles = tiles.reshape(chan_count, rows, 1, 2 * block_width)
    received = lax.all_to_all(tiles, "chan", split_axis=0, concat_axis=2, tiled=True)
    stacked = unshuffle_stage(received.reshape(rows, chan_count, 2 * block_width))
    return stacked.reshape(ROUNDS, 2, block_width, block_width, per_piece * chan_count)

def solution(mesh):
    return jax.shard_map(
        on_device,
        mesh=mesh,
        in_specs=(P("tm", "chan", None), P()),
        out_specs=P(None, None, "chan", None, "tm"),
        check_vma=False,
    )
```

```python
import functools
import math

import jax
import ml_dtypes
import numpy as np
import jax.numpy as jnp
from jax import lax
from jax.experimental import pallas as pl
from jax.experimental.pallas import tpu as pltpu
from jax.sharding import PartitionSpec as P

F = 512
L = 2048
ROUNDS = 2


def band_table(chan_count, day_count):
    per_piece = F // (chan_count * day_count)
    row_ids = np.arange(2 * F, dtype=np.int64)
    piece_idx = row_ids // (day_count * 2 * per_piece)
    remainder = row_ids % (day_count * 2 * per_piece)
    group_idx = remainder // (2 * per_piece)
    within = remainder % (2 * per_piece)
    imag_flag = within // per_piece
    offset_idx = within % per_piece
    freq_ids = group_idx * (chan_count * per_piece) + offset_idx * chan_count + piece_idx
    samples = np.arange(L, dtype=np.int64)
    angles = ((freq_ids[:, None] + 1) * samples[None, :] % L) * (2.0 * np.pi / L)
    taper_vals = 0.5 - 0.5 * np.cos((samples + 0.5) * (2.0 * np.pi / L))
    values = np.where(imag_flag[:, None] == 0, np.cos(angles), -np.sin(angles)) * taper_vals[None]
    return jnp.asarray(values.astype(ml_dtypes.bfloat16))

def pair_kernel(pair_ref, x_ref, o_ref, *, group, day_count, half, width, scale_value):
    step = pl.program_id(0)
    rows = 2 * 2 * half
    row_part = lax.broadcasted_iota(jnp.int32, (rows, 2 * width), 0) // (2 * half)
    lane_part = lax.broadcasted_iota(jnp.int32, (rows, 2 * width), 1) // width
    diagonal = row_part == lane_part

    def spread(part):
        stacked = jnp.concatenate([part, part], axis=0)
        return jnp.where(diagonal, stacked, jnp.zeros_like(stacked))

    def body(k, carry):
        block = step * group + k
        partners = [pair_ref[r, block] for r in range(ROUNDS)]
        accs = [jnp.zeros((width, 4 * width), jnp.float32) for _ in range(ROUNDS)]
        for day in range(day_count):
            own = x_ref[block, day]
            lhs = jnp.concatenate([own[:, :width], own[:, width:]], axis=0)
            for r in range(ROUNDS):
                other = x_ref[partners[r], day]
                rotated = jnp.concatenate([-other[half:], other[:half]], axis=0)
                rhs = jnp.concatenate([spread(other), spread(rotated)], axis=1)
                prod = lax.dot_general(
                    lhs, rhs, (((0,), (0,)), ((), ())), preferred_element_type=jnp.float32
                )
                accs[r] = accs[r] + prod.astype(jnp.bfloat16).astype(jnp.float32)
        for r in range(ROUNDS):
            scaled = (accs[r] * scale_value).astype(jnp.bfloat16)
            o_ref[k, r, 0] = scaled[:, :2 * width]
            o_ref[k, r, 1] = scaled[:, 2 * width:]
        return carry

    lax.fori_loop(0, group, body, 0)


def pair_stage(pairings, spectra, scale_value):
    block_count, day_count, rows, lanes = spectra.shape
    width = lanes // 2
    group = 8
    kernel = functools.partial(
        pair_kernel, group=group, day_count=day_count, half=rows // 2, width=width,
        scale_value=scale_value,
    )
    return pl.pallas_call(
        kernel,
        grid_spec=pltpu.PrefetchScalarGridSpec(
            num_scalar_prefetch=1,
            grid=(block_count // group,),
            in_specs=[pl.BlockSpec(spectra.shape, lambda i, pr: (0, 0, 0, 0))],
            out_specs=pl.BlockSpec(
                (group, ROUNDS, 2, width, lanes), lambda i, pr: (i, 0, 0, 0, 0)
            ),
        ),
        out_shape=jax.ShapeDtypeStruct((block_count, ROUNDS, 2, width, lanes), jnp.bfloat16),
    )(pairings, spectra)

def regroup_kernel(x_ref, o_ref, *, group, width):
    lane = lax.broadcasted_iota(jnp.int32, x_ref.shape[2:], 1)
    low_lanes = lane < width
    for g in range(group):
        for q in range(2):
            real_off = x_ref[g, 2 * q].astype(jnp.float32)
            imag_off = x_ref[g, 2 * q + 1].astype(jnp.float32)
            even = jnp.where(low_lanes, real_off, pltpu.roll(imag_off, width, 1))
            odd = jnp.where(low_lanes, pltpu.roll(real_off, width, 1), imag_off)
            rows = jnp.concatenate([even, odd], axis=0).astype(o_ref.dtype)
            o_ref[g, pl.ds(q * rows.shape[0], rows.shape[0])] = rows


def regroup_stage(pooled):
    units, parts, chunks, lanes = pooled.shape
    group = 8
    kernel = functools.partial(regroup_kernel, group=group, width=lanes // 2)
    out_rows = parts * chunks
    return pl.pallas_call(
        kernel,
        grid=(units // group,),
        in_specs=[pl.BlockSpec((group, parts, chunks, lanes), lambda i: (i, 0, 0, 0))],
        out_specs=pl.BlockSpec((group, out_rows, lanes), lambda i: (i, 0, 0)),
        out_shape=jax.ShapeDtypeStruct((units, out_rows, lanes), pooled.dtype),
    )(pooled)


def unshuffle_kernel(x_ref, o_ref, *, group, width):
    for k in range(group):
        flipped = x_ref[k].astype(jnp.float32).T
        o_ref[k] = jnp.concatenate([flipped[:width], flipped[width:]], axis=1).astype(o_ref.dtype)


def unshuffle_stage(received):
    rows, sources, lanes = received.shape
    group = 16
    kernel = functools.partial(unshuffle_kernel, group=group, width=lanes // 2)
    return pl.pallas_call(
        kernel,
        grid=(rows // group,),
        in_specs=[pl.BlockSpec((group, sources, lanes), lambda i: (i, 0, 0))],
        out_specs=pl.BlockSpec((group, lanes // 2, 2 * sources), lambda i: (i, 0, 0)),
        out_shape=jax.ShapeDtypeStruct((rows, lanes // 2, 2 * sources), jnp.bfloat16),
    )(received)


def on_device(raw_windows, pairings):
    win_count, block_width, length = raw_windows.shape
    chan_count = lax.axis_size("chan")
    day_count = lax.axis_size("tm")
    per_piece = F // (chan_count * day_count)
    dft_table = band_table(chan_count, day_count)
    flat_raw = raw_windows.reshape(win_count * block_width, length)
    spectra = lax.dot_general(
        dft_table, flat_raw, (((1,), (1,)), ((), ())), preferred_element_type=jnp.float32
    )
    power_sum = jnp.sum(spectra * spectra, axis=0) / F
    whitened = (spectra * lax.rsqrt(power_sum + 1e-06)[None, :]).astype(jnp.bfloat16)
    layered = whitened.reshape(chan_count * day_count, 2 * per_piece, win_count * block_width)
    scale_value = 1.0 / math.sqrt(win_count * day_count)
    pooled = lax.all_to_all(layered, ("chan", "tm"), split_axis=0, concat_axis=0, tiled=True)
    lanes = per_piece * block_width
    split = pooled.reshape(chan_count * day_count, 2 * per_piece, win_count * block_width // lanes, lanes)
    by_block = regroup_stage(split).reshape(chan_count, day_count, 2 * win_count, lanes)
    tiles = pair_stage(pairings, by_block, scale_value)
    rows = ROUNDS * 2 * block_width
    tiles = tiles.reshape(chan_count, rows, 1, 2 * block_width)
    received = lax.all_to_all(tiles, "chan", split_axis=0, concat_axis=2, tiled=True)
    stacked = unshuffle_stage(received.reshape(rows, chan_count, 2 * block_width))
    return stacked.reshape(ROUNDS, 2, block_width, block_width, per_piece * chan_count)

def solution(mesh):
    return jax.shard_map(
        on_device,
        mesh=mesh,
        in_specs=(P("tm", "chan", None), P()),
        out_specs=P(None, None, "chan", None, "tm"),
        check_vma=False,
    )
```

```python
import functools
import math

import jax
import ml_dtypes
import numpy as np
import jax.numpy as jnp
from jax import lax
from jax.experimental import pallas as pl
from jax.experimental.pallas import tpu as pltpu
from jax.sharding import PartitionSpec as P

F = 512
L = 2048
ROUNDS = 2


def band_table(chan_count, day_count):
    per_piece = F // (chan_count * day_count)
    row_ids = np.arange(2 * F, dtype=np.int64)
    piece_idx = row_ids // (day_count * 2 * per_piece)
    remainder = row_ids % (day_count * 2 * per_piece)
    group_idx = remainder // (2 * per_piece)
    within = remainder % (2 * per_piece)
    imag_flag = within // per_piece
    offset_idx = within % per_piece
    freq_ids = group_idx * (chan_count * per_piece) + offset_idx * chan_count + piece_idx
    samples = np.arange(L, dtype=np.int64)
    angles = ((freq_ids[:, None] + 1) * samples[None, :] % L) * (2.0 * np.pi / L)
    taper_vals = 0.5 - 0.5 * np.cos((samples + 0.5) * (2.0 * np.pi / L))
    values = np.where(imag_flag[:, None] == 0, np.cos(angles), -np.sin(angles)) * taper_vals[None]
    return jnp.asarray(values.astype(ml_dtypes.bfloat16))

def pair_kernel(pair_ref, x_ref, o_ref, *, group, day_count, half, width, scale_value):
    step = pl.program_id(0)
    rows = 2 * 2 * half
    row_part = lax.broadcasted_iota(jnp.int32, (rows, 2 * width), 0) // (2 * half)
    lane_part = lax.broadcasted_iota(jnp.int32, (rows, 2 * width), 1) // width
    diagonal = row_part == lane_part

    def spread(part):
        stacked = jnp.concatenate([part, part], axis=0)
        return jnp.where(diagonal, stacked, jnp.zeros_like(stacked))

    def body(k, carry):
        block = step * group + k
        partners = [pair_ref[r, block] for r in range(ROUNDS)]
        accs = [jnp.zeros((width, 4 * width), jnp.float32) for _ in range(ROUNDS)]
        for day in range(day_count):
            own = x_ref[block, day]
            lhs = jnp.concatenate([own[:, :width], own[:, width:]], axis=0)
            for r in range(ROUNDS):
                other = x_ref[partners[r], day]
                rotated = jnp.concatenate([-other[half:], other[:half]], axis=0)
                rhs = jnp.concatenate([spread(other), spread(rotated)], axis=1)
                prod = lax.dot_general(
                    lhs, rhs, (((0,), (0,)), ((), ())), preferred_element_type=jnp.float32
                )
                accs[r] = accs[r] + prod.astype(jnp.bfloat16).astype(jnp.float32)
        for r in range(ROUNDS):
            scaled = (accs[r] * scale_value).astype(jnp.bfloat16)
            o_ref[k, r, 0] = scaled[:, :2 * width]
            o_ref[k, r, 1] = scaled[:, 2 * width:]
        return carry

    lax.fori_loop(0, group, body, 0)


def pair_stage(pairings, spectra, scale_value):
    block_count, day_count, rows, lanes = spectra.shape
    width = lanes // 2
    group = 8
    kernel = functools.partial(
        pair_kernel, group=group, day_count=day_count, half=rows // 2, width=width,
        scale_value=scale_value,
    )
    return pl.pallas_call(
        kernel,
        grid_spec=pltpu.PrefetchScalarGridSpec(
            num_scalar_prefetch=1,
            grid=(block_count // group,),
            in_specs=[pl.BlockSpec(spectra.shape, lambda i, pr: (0, 0, 0, 0))],
            out_specs=pl.BlockSpec(
                (group, ROUNDS, 2, width, lanes), lambda i, pr: (i, 0, 0, 0, 0)
            ),
        ),
        out_shape=jax.ShapeDtypeStruct((block_count, ROUNDS, 2, width, lanes), jnp.bfloat16),
    )(pairings, spectra)

def regroup_kernel(x_ref, o_ref, *, group, width):
    lane = lax.broadcasted_iota(jnp.int32, x_ref.shape[2:], 1)
    low_lanes = lane < width

    def body(g, carry):
        for q in range(2):
            real_off = x_ref[g, 2 * q].astype(jnp.float32)
            imag_off = x_ref[g, 2 * q + 1].astype(jnp.float32)
            even = jnp.where(low_lanes, real_off, pltpu.roll(imag_off, width, 1))
            odd = jnp.where(low_lanes, pltpu.roll(real_off, width, 1), imag_off)
            rows = jnp.concatenate([even, odd], axis=0).astype(o_ref.dtype)
            o_ref[g, pl.ds(q * rows.shape[0], rows.shape[0])] = rows
        return carry

    lax.fori_loop(0, group, body, 0, unroll=4)


def regroup_stage(pooled):
    units, parts, chunks, lanes = pooled.shape
    group = 32
    kernel = functools.partial(regroup_kernel, group=group, width=lanes // 2)
    out_rows = parts * chunks
    return pl.pallas_call(
        kernel,
        grid=(units // group,),
        in_specs=[pl.BlockSpec((group, parts, chunks, lanes), lambda i: (i, 0, 0, 0))],
        out_specs=pl.BlockSpec((group, out_rows, lanes), lambda i: (i, 0, 0)),
        out_shape=jax.ShapeDtypeStruct((units, out_rows, lanes), pooled.dtype),
    )(pooled)


def unshuffle_kernel(x_ref, o_ref, *, group, width):
    def body(k, carry):
        flipped = x_ref[k].astype(jnp.float32).T
        o_ref[k] = jnp.concatenate([flipped[:width], flipped[width:]], axis=1).astype(o_ref.dtype)
        return carry

    lax.fori_loop(0, group, body, 0, unroll=4)


def unshuffle_stage(received):
    rows, sources, lanes = received.shape
    group = 64
    kernel = functools.partial(unshuffle_kernel, group=group, width=lanes // 2)
    return pl.pallas_call(
        kernel,
        grid=(rows // group,),
        in_specs=[pl.BlockSpec((group, sources, lanes), lambda i: (i, 0, 0))],
        out_specs=pl.BlockSpec((group, lanes // 2, 2 * sources), lambda i: (i, 0, 0)),
        out_shape=jax.ShapeDtypeStruct((rows, lanes // 2, 2 * sources), jnp.bfloat16),
    )(received)


def on_device(raw_windows, pairings):
    win_count, block_width, length = raw_windows.shape
    chan_count = lax.axis_size("chan")
    day_count = lax.axis_size("tm")
    per_piece = F // (chan_count * day_count)
    dft_table = band_table(chan_count, day_count)
    flat_raw = raw_windows.reshape(win_count * block_width, length)
    spectra = lax.dot_general(
        dft_table, flat_raw, (((1,), (1,)), ((), ())), preferred_element_type=jnp.float32
    )
    power_sum = jnp.sum(spectra * spectra, axis=0) / F
    whitened = (spectra * lax.rsqrt(power_sum + 1e-06)[None, :]).astype(jnp.bfloat16)
    layered = whitened.reshape(chan_count * day_count, 2 * per_piece, win_count * block_width)
    scale_value = 1.0 / math.sqrt(win_count * day_count)
    pooled = lax.all_to_all(layered, ("chan", "tm"), split_axis=0, concat_axis=0, tiled=True)
    lanes = per_piece * block_width
    split = pooled.reshape(chan_count * day_count, 2 * per_piece, win_count * block_width // lanes, lanes)
    by_block = regroup_stage(split).reshape(chan_count, day_count, 2 * win_count, lanes)
    tiles = pair_stage(pairings, by_block, scale_value)
    rows = ROUNDS * 2 * block_width
    tiles = tiles.reshape(chan_count, rows, 1, 2 * block_width)
    received = lax.all_to_all(tiles, "chan", split_axis=0, concat_axis=2, tiled=True)
    stacked = unshuffle_stage(received.reshape(rows, chan_count, 2 * block_width))
    return stacked.reshape(ROUNDS, 2, block_width, block_width, per_piece * chan_count)

def solution(mesh):
    return jax.shard_map(
        on_device,
        mesh=mesh,
        in_specs=(P("tm", "chan", None), P()),
        out_specs=P(None, None, "chan", None, "tm"),
        check_vma=False,
    )
```

```python
import functools
import math

import jax
import ml_dtypes
import numpy as np
import jax.numpy as jnp
from jax import lax
from jax.experimental import pallas as pl
from jax.experimental.pallas import tpu as pltpu
from jax.sharding import PartitionSpec as P

F = 512
L = 2048
ROUNDS = 2


def band_table(chan_count, day_count):
    per_piece = F // (chan_count * day_count)
    row_ids = np.arange(2 * F, dtype=np.int64)
    piece_idx = row_ids // (day_count * 2 * per_piece)
    remainder = row_ids % (day_count * 2 * per_piece)
    group_idx = remainder // (2 * per_piece)
    within = remainder % (2 * per_piece)
    imag_flag = within // per_piece
    offset_idx = within % per_piece
    freq_ids = group_idx * (chan_count * per_piece) + offset_idx * chan_count + piece_idx
    samples = np.arange(L, dtype=np.int64)
    angles = ((freq_ids[:, None] + 1) * samples[None, :] % L) * (2.0 * np.pi / L)
    taper_vals = 0.5 - 0.5 * np.cos((samples + 0.5) * (2.0 * np.pi / L))
    values = np.where(imag_flag[:, None] == 0, np.cos(angles), -np.sin(angles)) * taper_vals[None]
    return jnp.asarray(values.astype(ml_dtypes.bfloat16))

def pair_kernel(pair_ref, x_ref, o_ref, *, group, day_count, half, width, scale_value):
    step = pl.program_id(0)
    rows = 2 * 2 * half
    row_part = lax.broadcasted_iota(jnp.int32, (rows, 2 * width), 0) // (2 * half)
    lane_part = lax.broadcasted_iota(jnp.int32, (rows, 2 * width), 1) // width
    diagonal = row_part == lane_part

    def spread(part):
        stacked = jnp.concatenate([part, part], axis=0)
        return jnp.where(diagonal, stacked, jnp.zeros_like(stacked))

    def body(k, carry):
        block = step * group + k
        partners = [pair_ref[r, block] for r in range(ROUNDS)]
        accs = [jnp.zeros((width, 4 * width), jnp.float32) for _ in range(ROUNDS)]
        for day in range(day_count):
            own = x_ref[block, day]
            lhs = jnp.concatenate([own[:, :width], own[:, width:]], axis=0)
            for r in range(ROUNDS):
                other = x_ref[partners[r], day]
                rotated = jnp.concatenate([-other[half:], other[:half]], axis=0)
                rhs = jnp.concatenate([spread(other), spread(rotated)], axis=1)
                prod = lax.dot_general(
                    lhs, rhs, (((0,), (0,)), ((), ())), preferred_element_type=jnp.float32
                )
                accs[r] = accs[r] + prod.astype(jnp.bfloat16).astype(jnp.float32)
        for r in range(ROUNDS):
            scaled = (accs[r] * scale_value).astype(jnp.bfloat16)
            o_ref[k, r, 0] = scaled[:, :2 * width]
            o_ref[k, r, 1] = scaled[:, 2 * width:]
        return carry

    lax.fori_loop(0, group, body, 0)


def pair_stage(pairings, spectra, scale_value):
    block_count, day_count, rows, lanes = spectra.shape
    width = lanes // 2
    group = 8
    kernel = functools.partial(
        pair_kernel, group=group, day_count=day_count, half=rows // 2, width=width,
        scale_value=scale_value,
    )
    return pl.pallas_call(
        kernel,
        grid_spec=pltpu.PrefetchScalarGridSpec(
            num_scalar_prefetch=1,
            grid=(block_count // group,),
            in_specs=[pl.BlockSpec(spectra.shape, lambda i, pr: (0, 0, 0, 0))],
            out_specs=pl.BlockSpec(
                (group, ROUNDS, 2, width, lanes), lambda i, pr: (i, 0, 0, 0, 0)
            ),
        ),
        out_shape=jax.ShapeDtypeStruct((block_count, ROUNDS, 2, width, lanes), jnp.bfloat16),
    )(pairings, spectra)

def regroup_kernel(x_ref, o_ref, *, group, width):
    lane = lax.broadcasted_iota(jnp.int32, x_ref.shape[2:], 1)
    low_lanes = lane < width

    def body(g, carry):
        for q in range(2):
            real_off = x_ref[g, 2 * q].astype(jnp.float32)
            imag_off = x_ref[g, 2 * q + 1].astype(jnp.float32)
            even = jnp.where(low_lanes, real_off, pltpu.roll(imag_off, width, 1))
            odd = jnp.where(low_lanes, pltpu.roll(real_off, width, 1), imag_off)
            rows = jnp.concatenate([even, odd], axis=0).astype(o_ref.dtype)
            o_ref[g, pl.ds(q * rows.shape[0], rows.shape[0])] = rows
        return carry

    lax.fori_loop(0, group, body, 0, unroll=4)


def regroup_stage(pooled):
    units, parts, chunks, lanes = pooled.shape
    group = 32
    kernel = functools.partial(regroup_kernel, group=group, width=lanes // 2)
    out_rows = parts * chunks
    return pl.pallas_call(
        kernel,
        grid=(units // group,),
        in_specs=[pl.BlockSpec((group, parts, chunks, lanes), lambda i: (i, 0, 0, 0))],
        out_specs=pl.BlockSpec((group, out_rows, lanes), lambda i: (i, 0, 0)),
        out_shape=jax.ShapeDtypeStruct((units, out_rows, lanes), pooled.dtype),
    )(pooled)


def unshuffle_kernel(x_ref, o_ref, *, group, width):
    for k in range(group):
        flipped = x_ref[k].astype(jnp.float32).T
        o_ref[k] = jnp.concatenate([flipped[:width], flipped[width:]], axis=1).astype(o_ref.dtype)


def unshuffle_stage(received):
    rows, sources, lanes = received.shape
    group = 16
    kernel = functools.partial(unshuffle_kernel, group=group, width=lanes // 2)
    return pl.pallas_call(
        kernel,
        grid=(rows // group,),
        in_specs=[pl.BlockSpec((group, sources, lanes), lambda i: (i, 0, 0))],
        out_specs=pl.BlockSpec((group, lanes // 2, 2 * sources), lambda i: (i, 0, 0)),
        out_shape=jax.ShapeDtypeStruct((rows, lanes // 2, 2 * sources), jnp.bfloat16),
    )(received)


def on_device(raw_windows, pairings):
    win_count, block_width, length = raw_windows.shape
    chan_count = lax.axis_size("chan")
    day_count = lax.axis_size("tm")
    per_piece = F // (chan_count * day_count)
    dft_table = band_table(chan_count, day_count)
    flat_raw = raw_windows.reshape(win_count * block_width, length)
    spectra = lax.dot_general(
        dft_table, flat_raw, (((1,), (1,)), ((), ())), preferred_element_type=jnp.float32
    )
    power_sum = jnp.sum(spectra * spectra, axis=0) / F
    whitened = (spectra * lax.rsqrt(power_sum + 1e-06)[None, :]).astype(jnp.bfloat16)
    layered = whitened.reshape(chan_count * day_count, 2 * per_piece, win_count * block_width)
    scale_value = 1.0 / math.sqrt(win_count * day_count)
    pooled = lax.all_to_all(layered, ("chan", "tm"), split_axis=0, concat_axis=0, tiled=True)
    lanes = per_piece * block_width
    split = pooled.reshape(chan_count * day_count, 2 * per_piece, win_count * block_width // lanes, lanes)
    by_block = regroup_stage(split).reshape(chan_count, day_count, 2 * win_count, lanes)
    tiles = pair_stage(pairings, by_block, scale_value)
    rows = ROUNDS * 2 * block_width
    tiles = tiles.reshape(chan_count, rows, 1, 2 * block_width)
    received = lax.all_to_all(tiles, "chan", split_axis=0, concat_axis=2, tiled=True)
    stacked = unshuffle_stage(received.reshape(rows, chan_count, 2 * block_width))
    return stacked.reshape(ROUNDS, 2, block_width, block_width, per_piece * chan_count)

def solution(mesh):
    return jax.shard_map(
        on_device,
        mesh=mesh,
        in_specs=(P("tm", "chan", None), P()),
        out_specs=P(None, None, "chan", None, "tm"),
        check_vma=False,
    )
```

```python
import functools
import math

import jax
import ml_dtypes
import numpy as np
import jax.numpy as jnp
from jax import lax
from jax.experimental import pallas as pl
from jax.experimental.pallas import tpu as pltpu
from jax.sharding import PartitionSpec as P

F = 512
L = 2048
ROUNDS = 2


def band_table(chan_count, day_count):
    per_piece = F // (chan_count * day_count)
    row_ids = np.arange(2 * F, dtype=np.int64)
    piece_idx = row_ids // (day_count * 2 * per_piece)
    remainder = row_ids % (day_count * 2 * per_piece)
    group_idx = remainder // (2 * per_piece)
    within = remainder % (2 * per_piece)
    imag_flag = within // per_piece
    offset_idx = within % per_piece
    freq_ids = group_idx * (chan_count * per_piece) + offset_idx * chan_count + piece_idx
    samples = np.arange(L, dtype=np.int64)
    angles = ((freq_ids[:, None] + 1) * samples[None, :] % L) * (2.0 * np.pi / L)
    taper_vals = 0.5 - 0.5 * np.cos((samples + 0.5) * (2.0 * np.pi / L))
    values = np.where(imag_flag[:, None] == 0, np.cos(angles), -np.sin(angles)) * taper_vals[None]
    return jnp.asarray(values.astype(ml_dtypes.bfloat16))

def pair_kernel(pair_ref, x_ref, o_ref, *, group, day_count, half, width, scale_value):
    step = pl.program_id(0)
    rows = 2 * 2 * half
    row_part = lax.broadcasted_iota(jnp.int32, (rows, 2 * width), 0) // (2 * half)
    lane_part = lax.broadcasted_iota(jnp.int32, (rows, 2 * width), 1) // width
    diagonal = row_part == lane_part

    def spread(part):
        stacked = jnp.concatenate([part, part], axis=0)
        return jnp.where(diagonal, stacked, jnp.zeros_like(stacked))

    def body(k, carry):
        block = step * group + k
        partners = [pair_ref[r, block] for r in range(ROUNDS)]
        accs = [jnp.zeros((width, 4 * width), jnp.float32) for _ in range(ROUNDS)]
        for day in range(day_count):
            own = x_ref[block, day]
            lhs = jnp.concatenate([own[:, :width], own[:, width:]], axis=0)
            for r in range(ROUNDS):
                other = x_ref[partners[r], day]
                rotated = jnp.concatenate([-other[half:], other[:half]], axis=0)
                rhs = jnp.concatenate([spread(other), spread(rotated)], axis=1)
                prod = lax.dot_general(
                    lhs, rhs, (((0,), (0,)), ((), ())), preferred_element_type=jnp.float32
                )
                accs[r] = accs[r] + prod.astype(jnp.bfloat16).astype(jnp.float32)
        for r in range(ROUNDS):
            scaled = (accs[r] * scale_value).astype(jnp.bfloat16)
            o_ref[k, r, 0] = scaled[:, :2 * width]
            o_ref[k, r, 1] = scaled[:, 2 * width:]
        return carry

    lax.fori_loop(0, group, body, 0)


def pair_stage(pairings, spectra, scale_value):
    block_count, day_count, rows, lanes = spectra.shape
    width = lanes // 2
    group = 8
    kernel = functools.partial(
        pair_kernel, group=group, day_count=day_count, half=rows // 2, width=width,
        scale_value=scale_value,
    )
    return pl.pallas_call(
        kernel,
        grid_spec=pltpu.PrefetchScalarGridSpec(
            num_scalar_prefetch=1,
            grid=(block_count // group,),
            in_specs=[pl.BlockSpec(spectra.shape, lambda i, pr: (0, 0, 0, 0))],
            out_specs=pl.BlockSpec(
                (group, ROUNDS, 2, width, lanes), lambda i, pr: (i, 0, 0, 0, 0)
            ),
        ),
        out_shape=jax.ShapeDtypeStruct((block_count, ROUNDS, 2, width, lanes), jnp.bfloat16),
    )(pairings, spectra)

def regroup_kernel(x_ref, o_ref, *, group, width):
    lane = lax.broadcasted_iota(jnp.int32, x_ref.shape[2:], 1)
    low_lanes = lane < width

    def body(g, carry):
        for q in range(2):
            real_off = x_ref[g, 2 * q].astype(jnp.float32)
            imag_off = x_ref[g, 2 * q + 1].astype(jnp.float32)
            even = jnp.where(low_lanes, real_off, pltpu.roll(imag_off, width, 1))
            odd = jnp.where(low_lanes, pltpu.roll(real_off, width, 1), imag_off)
            rows = jnp.concatenate([even, odd], axis=0).astype(o_ref.dtype)
            o_ref[g, pl.ds(q * rows.shape[0], rows.shape[0])] = rows
        return carry

    lax.fori_loop(0, group, body, 0, unroll=4)


def regroup_stage(pooled):
    units, parts, chunks, lanes = pooled.shape
    group = 32
    kernel = functools.partial(regroup_kernel, group=group, width=lanes // 2)
    out_rows = parts * chunks
    return pl.pallas_call(
        kernel,
        grid=(units // group,),
        in_specs=[pl.BlockSpec((group, parts, chunks, lanes), lambda i: (i, 0, 0, 0))],
        out_specs=pl.BlockSpec((group, out_rows, lanes), lambda i: (i, 0, 0)),
        out_shape=jax.ShapeDtypeStruct((units, out_rows, lanes), pooled.dtype),
    )(pooled)


def unshuffle_kernel(x_ref, o_ref, *, group, width):
    for k in range(group):
        flipped = x_ref[k].T
        o_ref[k] = jnp.concatenate([flipped[:width], flipped[width:]], axis=1).astype(o_ref.dtype)


def unshuffle_stage(received):
    rows, sources, lanes = received.shape
    group = 16
    kernel = functools.partial(unshuffle_kernel, group=group, width=lanes // 2)
    return pl.pallas_call(
        kernel,
        grid=(rows // group,),
        in_specs=[pl.BlockSpec((group, sources, lanes), lambda i: (i, 0, 0))],
        out_specs=pl.BlockSpec((group, lanes // 2, 2 * sources), lambda i: (i, 0, 0)),
        out_shape=jax.ShapeDtypeStruct((rows, lanes // 2, 2 * sources), jnp.bfloat16),
    )(received)


def on_device(raw_windows, pairings):
    win_count, block_width, length = raw_windows.shape
    chan_count = lax.axis_size("chan")
    day_count = lax.axis_size("tm")
    per_piece = F // (chan_count * day_count)
    dft_table = band_table(chan_count, day_count)
    flat_raw = raw_windows.reshape(win_count * block_width, length)
    spectra = lax.dot_general(
        dft_table, flat_raw, (((1,), (1,)), ((), ())), preferred_element_type=jnp.float32
    )
    power_sum = jnp.sum(spectra * spectra, axis=0) / F
    whitened = (spectra * lax.rsqrt(power_sum + 1e-06)[None, :]).astype(jnp.bfloat16)
    layered = whitened.reshape(chan_count * day_count, 2 * per_piece, win_count * block_width)
    scale_value = 1.0 / math.sqrt(win_count * day_count)
    pooled = lax.all_to_all(layered, ("chan", "tm"), split_axis=0, concat_axis=0, tiled=True)
    lanes = per_piece * block_width
    split = pooled.reshape(chan_count * day_count, 2 * per_piece, win_count * block_width // lanes, lanes)
    by_block = regroup_stage(split).reshape(chan_count, day_count, 2 * win_count, lanes)
    tiles = pair_stage(pairings, by_block, scale_value)
    rows = ROUNDS * 2 * block_width
    tiles = tiles.reshape(chan_count, rows, 1, 2 * block_width)
    received = lax.all_to_all(tiles, "chan", split_axis=0, concat_axis=2, tiled=True)
    stacked = unshuffle_stage(received.reshape(rows, chan_count, 2 * block_width))
    return stacked.reshape(ROUNDS, 2, block_width, block_width, per_piece * chan_count)

def solution(mesh):
    return jax.shard_map(
        on_device,
        mesh=mesh,
        in_specs=(P("tm", "chan", None), P()),
        out_specs=P(None, None, "chan", None, "tm"),
        check_vma=False,
    )
```

```python
import functools
import math

import jax
import ml_dtypes
import numpy as np
import jax.numpy as jnp
from jax import lax
from jax.experimental import pallas as pl
from jax.experimental.pallas import tpu as pltpu
from jax.sharding import PartitionSpec as P

F = 512
L = 2048
ROUNDS = 2


def band_table(chan_count, day_count):
    per_piece = F // (chan_count * day_count)
    row_ids = np.arange(2 * F, dtype=np.int64)
    piece_idx = row_ids // (day_count * 2 * per_piece)
    remainder = row_ids % (day_count * 2 * per_piece)
    group_idx = remainder // (2 * per_piece)
    within = remainder % (2 * per_piece)
    imag_flag = within // per_piece
    offset_idx = within % per_piece
    freq_ids = group_idx * (chan_count * per_piece) + offset_idx * chan_count + piece_idx
    samples = np.arange(L, dtype=np.int64)
    angles = ((freq_ids[:, None] + 1) * samples[None, :] % L) * (2.0 * np.pi / L)
    taper_vals = 0.5 - 0.5 * np.cos((samples + 0.5) * (2.0 * np.pi / L))
    values = np.where(imag_flag[:, None] == 0, np.cos(angles), -np.sin(angles)) * taper_vals[None]
    return jnp.asarray(values.astype(ml_dtypes.bfloat16))

def pair_kernel(pair_ref, x_ref, o_ref, *, group, day_count, half, width, scale_value):
    step = pl.program_id(0)
    rows = 2 * 2 * half
    row_part = lax.broadcasted_iota(jnp.int32, (rows, 2 * width), 0) // (2 * half)
    lane_part = lax.broadcasted_iota(jnp.int32, (rows, 2 * width), 1) // width
    diagonal = row_part == lane_part

    def spread(part):
        stacked = jnp.concatenate([part, part], axis=0)
        return jnp.where(diagonal, stacked, jnp.zeros_like(stacked))

    def body(k, carry):
        block = step * group + k
        partners = [pair_ref[r, block] for r in range(ROUNDS)]
        accs = [jnp.zeros((width, 4 * width), jnp.float32) for _ in range(ROUNDS)]
        for day in range(day_count):
            own = x_ref[block, day]
            lhs = jnp.concatenate([own[:, :width], own[:, width:]], axis=0)
            for r in range(ROUNDS):
                other = x_ref[partners[r], day]
                rotated = jnp.concatenate([-other[half:], other[:half]], axis=0)
                rhs = jnp.concatenate([spread(other), spread(rotated)], axis=1)
                prod = lax.dot_general(
                    lhs, rhs, (((0,), (0,)), ((), ())), preferred_element_type=jnp.float32
                )
                accs[r] = accs[r] + prod.astype(jnp.bfloat16).astype(jnp.float32)
        for r in range(ROUNDS):
            scaled = (accs[r] * scale_value).astype(jnp.bfloat16)
            o_ref[k, r, 0] = scaled[:, :2 * width]
            o_ref[k, r, 1] = scaled[:, 2 * width:]
        return carry

    lax.fori_loop(0, group, body, 0, unroll=2)


def pair_stage(pairings, spectra, scale_value):
    block_count, day_count, rows, lanes = spectra.shape
    width = lanes // 2
    group = 8
    kernel = functools.partial(
        pair_kernel, group=group, day_count=day_count, half=rows // 2, width=width,
        scale_value=scale_value,
    )
    return pl.pallas_call(
        kernel,
        grid_spec=pltpu.PrefetchScalarGridSpec(
            num_scalar_prefetch=1,
            grid=(block_count // group,),
            in_specs=[pl.BlockSpec(spectra.shape, lambda i, pr: (0, 0, 0, 0))],
            out_specs=pl.BlockSpec(
                (group, ROUNDS, 2, width, lanes), lambda i, pr: (i, 0, 0, 0, 0)
            ),
        ),
        out_shape=jax.ShapeDtypeStruct((block_count, ROUNDS, 2, width, lanes), jnp.bfloat16),
    )(pairings, spectra)

def regroup_kernel(x_ref, o_ref, *, group, width):
    lane = lax.broadcasted_iota(jnp.int32, x_ref.shape[2:], 1)
    low_lanes = lane < width

    def body(g, carry):
        for q in range(2):
            real_off = x_ref[g, 2 * q].astype(jnp.float32)
            imag_off = x_ref[g, 2 * q + 1].astype(jnp.float32)
            even = jnp.where(low_lanes, real_off, pltpu.roll(imag_off, width, 1))
            odd = jnp.where(low_lanes, pltpu.roll(real_off, width, 1), imag_off)
            rows = jnp.concatenate([even, odd], axis=0).astype(o_ref.dtype)
            o_ref[g, pl.ds(q * rows.shape[0], rows.shape[0])] = rows
        return carry

    lax.fori_loop(0, group, body, 0, unroll=4)


def regroup_stage(pooled):
    units, parts, chunks, lanes = pooled.shape
    group = 32
    kernel = functools.partial(regroup_kernel, group=group, width=lanes // 2)
    out_rows = parts * chunks
    return pl.pallas_call(
        kernel,
        grid=(units // group,),
        in_specs=[pl.BlockSpec((group, parts, chunks, lanes), lambda i: (i, 0, 0, 0))],
        out_specs=pl.BlockSpec((group, out_rows, lanes), lambda i: (i, 0, 0)),
        out_shape=jax.ShapeDtypeStruct((units, out_rows, lanes), pooled.dtype),
    )(pooled)


def unshuffle_kernel(x_ref, o_ref, *, group, width):
    for k in range(group):
        flipped = x_ref[k].T
        o_ref[k] = jnp.concatenate([flipped[:width], flipped[width:]], axis=1).astype(o_ref.dtype)


def unshuffle_stage(received):
    rows, sources, lanes = received.shape
    group = 16
    kernel = functools.partial(unshuffle_kernel, group=group, width=lanes // 2)
    return pl.pallas_call(
        kernel,
        grid=(rows // group,),
        in_specs=[pl.BlockSpec((group, sources, lanes), lambda i: (i, 0, 0))],
        out_specs=pl.BlockSpec((group, lanes // 2, 2 * sources), lambda i: (i, 0, 0)),
        out_shape=jax.ShapeDtypeStruct((rows, lanes // 2, 2 * sources), jnp.bfloat16),
    )(received)


def on_device(raw_windows, pairings):
    win_count, block_width, length = raw_windows.shape
    chan_count = lax.axis_size("chan")
    day_count = lax.axis_size("tm")
    per_piece = F // (chan_count * day_count)
    dft_table = band_table(chan_count, day_count)
    flat_raw = raw_windows.reshape(win_count * block_width, length)
    spectra = lax.dot_general(
        dft_table, flat_raw, (((1,), (1,)), ((), ())), preferred_element_type=jnp.float32
    )
    power_sum = jnp.sum(spectra * spectra, axis=0) / F
    whitened = (spectra * lax.rsqrt(power_sum + 1e-06)[None, :]).astype(jnp.bfloat16)
    layered = whitened.reshape(chan_count * day_count, 2 * per_piece, win_count * block_width)
    scale_value = 1.0 / math.sqrt(win_count * day_count)
    pooled = lax.all_to_all(layered, ("chan", "tm"), split_axis=0, concat_axis=0, tiled=True)
    lanes = per_piece * block_width
    split = pooled.reshape(chan_count * day_count, 2 * per_piece, win_count * block_width // lanes, lanes)
    by_block = regroup_stage(split).reshape(chan_count, day_count, 2 * win_count, lanes)
    tiles = pair_stage(pairings, by_block, scale_value)
    rows = ROUNDS * 2 * block_width
    tiles = tiles.reshape(chan_count, rows, 1, 2 * block_width)
    received = lax.all_to_all(tiles, "chan", split_axis=0, concat_axis=2, tiled=True)
    stacked = unshuffle_stage(received.reshape(rows, chan_count, 2 * block_width))
    return stacked.reshape(ROUNDS, 2, block_width, block_width, per_piece * chan_count)

def solution(mesh):
    return jax.shard_map(
        on_device,
        mesh=mesh,
        in_specs=(P("tm", "chan", None), P()),
        out_specs=P(None, None, "chan", None, "tm"),
        check_vma=False,
    )
```

```python
import functools
import math

import jax
import ml_dtypes
import numpy as np
import jax.numpy as jnp
from jax import lax
from jax.experimental import pallas as pl
from jax.experimental.pallas import tpu as pltpu
from jax.sharding import PartitionSpec as P

F = 512
L = 2048
ROUNDS = 2


def band_table(chan_count, day_count):
    per_piece = F // (chan_count * day_count)
    row_ids = np.arange(2 * F, dtype=np.int64)
    piece_idx = row_ids // (day_count * 2 * per_piece)
    remainder = row_ids % (day_count * 2 * per_piece)
    group_idx = remainder // (2 * per_piece)
    within = remainder % (2 * per_piece)
    imag_flag = within // per_piece
    offset_idx = within % per_piece
    freq_ids = group_idx * (chan_count * per_piece) + offset_idx * chan_count + piece_idx
    samples = np.arange(L, dtype=np.int64)
    angles = ((freq_ids[:, None] + 1) * samples[None, :] % L) * (2.0 * np.pi / L)
    taper_vals = 0.5 - 0.5 * np.cos((samples + 0.5) * (2.0 * np.pi / L))
    values = np.where(imag_flag[:, None] == 0, np.cos(angles), -np.sin(angles)) * taper_vals[None]
    return jnp.asarray(values.astype(ml_dtypes.bfloat16))

def pair_kernel(pair_ref, x_ref, o_ref, *, group, day_count, half, width, scale_value):
    step = pl.program_id(0)
    rows = 2 * 2 * half
    row_part = lax.broadcasted_iota(jnp.int32, (rows, 2 * width), 0) // (2 * half)
    lane_part = lax.broadcasted_iota(jnp.int32, (rows, 2 * width), 1) // width
    diagonal = row_part == lane_part

    def spread(part):
        stacked = jnp.concatenate([part, part], axis=0)
        return jnp.where(diagonal, stacked, jnp.zeros_like(stacked))

    def body(k, carry):
        block = step * group + k
        partners = [pair_ref[r, block] for r in range(ROUNDS)]
        accs = [jnp.zeros((width, 4 * width), jnp.float32) for _ in range(ROUNDS)]
        for day in range(day_count):
            own = x_ref[block, day]
            lhs = jnp.concatenate([own[:, :width], own[:, width:]], axis=0)
            for r in range(ROUNDS):
                other = x_ref[partners[r], day]
                rotated = jnp.concatenate([-other[half:], other[:half]], axis=0)
                rhs = jnp.concatenate([spread(other), spread(rotated)], axis=1)
                prod = lax.dot_general(
                    lhs, rhs, (((0,), (0,)), ((), ())), preferred_element_type=jnp.float32
                )
                accs[r] = accs[r] + prod.astype(jnp.bfloat16).astype(jnp.float32)
        for r in range(ROUNDS):
            scaled = (accs[r] * scale_value).astype(jnp.bfloat16)
            o_ref[k, r, 0] = scaled[:, :2 * width]
            o_ref[k, r, 1] = scaled[:, 2 * width:]
        return carry

    lax.fori_loop(0, group, body, 0, unroll=4)


def pair_stage(pairings, spectra, scale_value):
    block_count, day_count, rows, lanes = spectra.shape
    width = lanes // 2
    group = 8
    kernel = functools.partial(
        pair_kernel, group=group, day_count=day_count, half=rows // 2, width=width,
        scale_value=scale_value,
    )
    return pl.pallas_call(
        kernel,
        grid_spec=pltpu.PrefetchScalarGridSpec(
            num_scalar_prefetch=1,
            grid=(block_count // group,),
            in_specs=[pl.BlockSpec(spectra.shape, lambda i, pr: (0, 0, 0, 0))],
            out_specs=pl.BlockSpec(
                (group, ROUNDS, 2, width, lanes), lambda i, pr: (i, 0, 0, 0, 0)
            ),
        ),
        out_shape=jax.ShapeDtypeStruct((block_count, ROUNDS, 2, width, lanes), jnp.bfloat16),
    )(pairings, spectra)

def regroup_kernel(x_ref, o_ref, *, group, width):
    lane = lax.broadcasted_iota(jnp.int32, x_ref.shape[2:], 1)
    low_lanes = lane < width

    def body(g, carry):
        for q in range(2):
            real_off = x_ref[g, 2 * q].astype(jnp.float32)
            imag_off = x_ref[g, 2 * q + 1].astype(jnp.float32)
            even = jnp.where(low_lanes, real_off, pltpu.roll(imag_off, width, 1))
            odd = jnp.where(low_lanes, pltpu.roll(real_off, width, 1), imag_off)
            rows = jnp.concatenate([even, odd], axis=0).astype(o_ref.dtype)
            o_ref[g, pl.ds(q * rows.shape[0], rows.shape[0])] = rows
        return carry

    lax.fori_loop(0, group, body, 0, unroll=4)


def regroup_stage(pooled):
    units, parts, chunks, lanes = pooled.shape
    group = 32
    kernel = functools.partial(regroup_kernel, group=group, width=lanes // 2)
    out_rows = parts * chunks
    return pl.pallas_call(
        kernel,
        grid=(units // group,),
        in_specs=[pl.BlockSpec((group, parts, chunks, lanes), lambda i: (i, 0, 0, 0))],
        out_specs=pl.BlockSpec((group, out_rows, lanes), lambda i: (i, 0, 0)),
        out_shape=jax.ShapeDtypeStruct((units, out_rows, lanes), pooled.dtype),
    )(pooled)


def unshuffle_kernel(x_ref, o_ref, *, group, width):
    for k in range(group):
        flipped = x_ref[k].T
        o_ref[k] = jnp.concatenate([flipped[:width], flipped[width:]], axis=1).astype(o_ref.dtype)


def unshuffle_stage(received):
    rows, sources, lanes = received.shape
    group = 16
    kernel = functools.partial(unshuffle_kernel, group=group, width=lanes // 2)
    return pl.pallas_call(
        kernel,
        grid=(rows // group,),
        in_specs=[pl.BlockSpec((group, sources, lanes), lambda i: (i, 0, 0))],
        out_specs=pl.BlockSpec((group, lanes // 2, 2 * sources), lambda i: (i, 0, 0)),
        out_shape=jax.ShapeDtypeStruct((rows, lanes // 2, 2 * sources), jnp.bfloat16),
    )(received)


def on_device(raw_windows, pairings):
    win_count, block_width, length = raw_windows.shape
    chan_count = lax.axis_size("chan")
    day_count = lax.axis_size("tm")
    per_piece = F // (chan_count * day_count)
    dft_table = band_table(chan_count, day_count)
    flat_raw = raw_windows.reshape(win_count * block_width, length)
    spectra = lax.dot_general(
        dft_table, flat_raw, (((1,), (1,)), ((), ())), preferred_element_type=jnp.float32
    )
    power_sum = jnp.sum(spectra * spectra, axis=0) / F
    whitened = (spectra * lax.rsqrt(power_sum + 1e-06)[None, :]).astype(jnp.bfloat16)
    layered = whitened.reshape(chan_count * day_count, 2 * per_piece, win_count * block_width)
    scale_value = 1.0 / math.sqrt(win_count * day_count)
    pooled = lax.all_to_all(layered, ("chan", "tm"), split_axis=0, concat_axis=0, tiled=True)
    lanes = per_piece * block_width
    split = pooled.reshape(chan_count * day_count, 2 * per_piece, win_count * block_width // lanes, lanes)
    by_block = regroup_stage(split).reshape(chan_count, day_count, 2 * win_count, lanes)
    tiles = pair_stage(pairings, by_block, scale_value)
    rows = ROUNDS * 2 * block_width
    tiles = tiles.reshape(chan_count, rows, 1, 2 * block_width)
    received = lax.all_to_all(tiles, "chan", split_axis=0, concat_axis=2, tiled=True)
    stacked = unshuffle_stage(received.reshape(rows, chan_count, 2 * block_width))
    return stacked.reshape(ROUNDS, 2, block_width, block_width, per_piece * chan_count)

def solution(mesh):
    return jax.shard_map(
        on_device,
        mesh=mesh,
        in_specs=(P("tm", "chan", None), P()),
        out_specs=P(None, None, "chan", None, "tm"),
        check_vma=False,
    )
```

```python
import functools
import math

import jax
import ml_dtypes
import numpy as np
import jax.numpy as jnp
from jax import lax
from jax.experimental import pallas as pl
from jax.experimental.pallas import tpu as pltpu
from jax.sharding import PartitionSpec as P

F = 512
L = 2048
ROUNDS = 2


def band_table(chan_count, day_count):
    per_piece = F // (chan_count * day_count)
    row_ids = np.arange(2 * F, dtype=np.int64)
    piece_idx = row_ids // (day_count * 2 * per_piece)
    remainder = row_ids % (day_count * 2 * per_piece)
    group_idx = remainder // (2 * per_piece)
    within = remainder % (2 * per_piece)
    imag_flag = within // per_piece
    offset_idx = within % per_piece
    freq_ids = group_idx * (chan_count * per_piece) + offset_idx * chan_count + piece_idx
    samples = np.arange(L, dtype=np.int64)
    angles = ((freq_ids[:, None] + 1) * samples[None, :] % L) * (2.0 * np.pi / L)
    taper_vals = 0.5 - 0.5 * np.cos((samples + 0.5) * (2.0 * np.pi / L))
    values = np.where(imag_flag[:, None] == 0, np.cos(angles), -np.sin(angles)) * taper_vals[None]
    return jnp.asarray(values.astype(ml_dtypes.bfloat16))

def pair_kernel(pair_ref, x_ref, o_ref, *, group, day_count, half, width, scale_value):
    step = pl.program_id(0)
    rows = 2 * 2 * half
    row_part = lax.broadcasted_iota(jnp.int32, (rows, 2 * width), 0) // (2 * half)
    lane_part = lax.broadcasted_iota(jnp.int32, (rows, 2 * width), 1) // width
    diagonal = row_part == lane_part

    def spread(part):
        stacked = jnp.concatenate([part, part], axis=0)
        return jnp.where(diagonal, stacked, jnp.zeros_like(stacked))

    def body(k, carry):
        block = step * group + k
        partners = [pair_ref[r, block] for r in range(ROUNDS)]
        accs = [jnp.zeros((width, 4 * width), jnp.float32) for _ in range(ROUNDS)]
        for day in range(day_count):
            own = x_ref[block, day]
            lhs = jnp.concatenate([own[:, :width], own[:, width:]], axis=0)
            for r in range(ROUNDS):
                other = x_ref[partners[r], day]
                rotated = jnp.concatenate([-other[half:], other[:half]], axis=0)
                rhs = jnp.concatenate([spread(other), spread(rotated)], axis=1)
                prod = lax.dot_general(
                    lhs, rhs, (((0,), (0,)), ((), ())), preferred_element_type=jnp.float32
                )
                accs[r] = accs[r] + prod.astype(jnp.bfloat16).astype(jnp.float32)
        for r in range(ROUNDS):
            scaled = (accs[r] * scale_value).astype(jnp.bfloat16)
            o_ref[k, r, 0] = scaled[:, :2 * width]
            o_ref[k, r, 1] = scaled[:, 2 * width:]
        return carry

    lax.fori_loop(0, group, body, 0, unroll=8)


def pair_stage(pairings, spectra, scale_value):
    block_count, day_count, rows, lanes = spectra.shape
    width = lanes // 2
    group = 8
    kernel = functools.partial(
        pair_kernel, group=group, day_count=day_count, half=rows // 2, width=width,
        scale_value=scale_value,
    )
    return pl.pallas_call(
        kernel,
        grid_spec=pltpu.PrefetchScalarGridSpec(
            num_scalar_prefetch=1,
            grid=(block_count // group,),
            in_specs=[pl.BlockSpec(spectra.shape, lambda i, pr: (0, 0, 0, 0))],
            out_specs=pl.BlockSpec(
                (group, ROUNDS, 2, width, lanes), lambda i, pr: (i, 0, 0, 0, 0)
            ),
        ),
        out_shape=jax.ShapeDtypeStruct((block_count, ROUNDS, 2, width, lanes), jnp.bfloat16),
    )(pairings, spectra)

def regroup_kernel(x_ref, o_ref, *, group, width):
    lane = lax.broadcasted_iota(jnp.int32, x_ref.shape[2:], 1)
    low_lanes = lane < width

    def body(g, carry):
        for q in range(2):
            real_off = x_ref[g, 2 * q].astype(jnp.float32)
            imag_off = x_ref[g, 2 * q + 1].astype(jnp.float32)
            even = jnp.where(low_lanes, real_off, pltpu.roll(imag_off, width, 1))
            odd = jnp.where(low_lanes, pltpu.roll(real_off, width, 1), imag_off)
            rows = jnp.concatenate([even, odd], axis=0).astype(o_ref.dtype)
            o_ref[g, pl.ds(q * rows.shape[0], rows.shape[0])] = rows
        return carry

    lax.fori_loop(0, group, body, 0, unroll=8)


def regroup_stage(pooled):
    units, parts, chunks, lanes = pooled.shape
    group = 32
    kernel = functools.partial(regroup_kernel, group=group, width=lanes // 2)
    out_rows = parts * chunks
    return pl.pallas_call(
        kernel,
        grid=(units // group,),
        in_specs=[pl.BlockSpec((group, parts, chunks, lanes), lambda i: (i, 0, 0, 0))],
        out_specs=pl.BlockSpec((group, out_rows, lanes), lambda i: (i, 0, 0)),
        out_shape=jax.ShapeDtypeStruct((units, out_rows, lanes), pooled.dtype),
    )(pooled)


def unshuffle_kernel(x_ref, o_ref, *, group, width):
    for k in range(group):
        flipped = x_ref[k].T
        o_ref[k] = jnp.concatenate([flipped[:width], flipped[width:]], axis=1).astype(o_ref.dtype)


def unshuffle_stage(received):
    rows, sources, lanes = received.shape
    group = 16
    kernel = functools.partial(unshuffle_kernel, group=group, width=lanes // 2)
    return pl.pallas_call(
        kernel,
        grid=(rows // group,),
        in_specs=[pl.BlockSpec((group, sources, lanes), lambda i: (i, 0, 0))],
        out_specs=pl.BlockSpec((group, lanes // 2, 2 * sources), lambda i: (i, 0, 0)),
        out_shape=jax.ShapeDtypeStruct((rows, lanes // 2, 2 * sources), jnp.bfloat16),
    )(received)


def on_device(raw_windows, pairings):
    win_count, block_width, length = raw_windows.shape
    chan_count = lax.axis_size("chan")
    day_count = lax.axis_size("tm")
    per_piece = F // (chan_count * day_count)
    dft_table = band_table(chan_count, day_count)
    flat_raw = raw_windows.reshape(win_count * block_width, length)
    spectra = lax.dot_general(
        dft_table, flat_raw, (((1,), (1,)), ((), ())), preferred_element_type=jnp.float32
    )
    power_sum = jnp.sum(spectra * spectra, axis=0) / F
    whitened = (spectra * lax.rsqrt(power_sum + 1e-06)[None, :]).astype(jnp.bfloat16)
    layered = whitened.reshape(chan_count * day_count, 2 * per_piece, win_count * block_width)
    scale_value = 1.0 / math.sqrt(win_count * day_count)
    pooled = lax.all_to_all(layered, ("chan", "tm"), split_axis=0, concat_axis=0, tiled=True)
    lanes = per_piece * block_width
    split = pooled.reshape(chan_count * day_count, 2 * per_piece, win_count * block_width // lanes, lanes)
    by_block = regroup_stage(split).reshape(chan_count, day_count, 2 * win_count, lanes)
    tiles = pair_stage(pairings, by_block, scale_value)
    rows = ROUNDS * 2 * block_width
    tiles = tiles.reshape(chan_count, rows, 1, 2 * block_width)
    received = lax.all_to_all(tiles, "chan", split_axis=0, concat_axis=2, tiled=True)
    stacked = unshuffle_stage(received.reshape(rows, chan_count, 2 * block_width))
    return stacked.reshape(ROUNDS, 2, block_width, block_width, per_piece * chan_count)

def solution(mesh):
    return jax.shard_map(
        on_device,
        mesh=mesh,
        in_specs=(P("tm", "chan", None), P()),
        out_specs=P(None, None, "chan", None, "tm"),
        check_vma=False,
    )
```

```python
import functools
import math

import jax
import ml_dtypes
import numpy as np
import jax.numpy as jnp
from jax import lax
from jax.experimental import pallas as pl
from jax.experimental.pallas import tpu as pltpu
from jax.sharding import PartitionSpec as P

F = 512
L = 2048
ROUNDS = 2


def band_table(chan_count, day_count):
    per_piece = F // (chan_count * day_count)
    row_ids = np.arange(2 * F, dtype=np.int64)
    piece_idx = row_ids // (day_count * 2 * per_piece)
    remainder = row_ids % (day_count * 2 * per_piece)
    group_idx = remainder // (2 * per_piece)
    within = remainder % (2 * per_piece)
    imag_flag = within // per_piece
    offset_idx = within % per_piece
    freq_ids = group_idx * (chan_count * per_piece) + offset_idx * chan_count + piece_idx
    samples = np.arange(L, dtype=np.int64)
    angles = ((freq_ids[:, None] + 1) * samples[None, :] % L) * (2.0 * np.pi / L)
    taper_vals = 0.5 - 0.5 * np.cos((samples + 0.5) * (2.0 * np.pi / L))
    values = np.where(imag_flag[:, None] == 0, np.cos(angles), -np.sin(angles)) * taper_vals[None]
    return jnp.asarray(values.astype(ml_dtypes.bfloat16))

def pair_kernel(pair_ref, x_ref, o_ref, *, group, day_count, half, width, scale_value):
    step = pl.program_id(0)
    rows = 2 * 2 * half
    row_part = lax.broadcasted_iota(jnp.int32, (rows, 2 * width), 0) // (2 * half)
    lane_part = lax.broadcasted_iota(jnp.int32, (rows, 2 * width), 1) // width
    diagonal = row_part == lane_part

    def spread(part):
        stacked = jnp.concatenate([part, part], axis=0)
        return jnp.where(diagonal, stacked, jnp.zeros_like(stacked))

    def body(k, carry):
        block = step * group + k
        partners = [pair_ref[r, block] for r in range(ROUNDS)]
        accs = [jnp.zeros((width, 4 * width), jnp.float32) for _ in range(ROUNDS)]
        for day in range(day_count):
            own = x_ref[block, day]
            lhs = jnp.concatenate([own[:, :width], own[:, width:]], axis=0)
            for r in range(ROUNDS):
                other = x_ref[partners[r], day]
                rotated = jnp.concatenate([-other[half:], other[:half]], axis=0)
                rhs = jnp.concatenate([spread(other), spread(rotated)], axis=1)
                prod = lax.dot_general(
                    lhs, rhs, (((0,), (0,)), ((), ())), preferred_element_type=jnp.float32
                )
                accs[r] = accs[r] + prod.astype(jnp.bfloat16).astype(jnp.float32)
        for r in range(ROUNDS):
            scaled = (accs[r] * scale_value).astype(jnp.bfloat16)
            o_ref[k, r, 0] = scaled[:, :2 * width]
            o_ref[k, r, 1] = scaled[:, 2 * width:]
        return carry

    lax.fori_loop(0, group, body, 0, unroll=8)


def pair_stage(pairings, spectra, scale_value):
    block_count, day_count, rows, lanes = spectra.shape
    width = lanes // 2
    group = 8
    kernel = functools.partial(
        pair_kernel, group=group, day_count=day_count, half=rows // 2, width=width,
        scale_value=scale_value,
    )
    return pl.pallas_call(
        kernel,
        grid_spec=pltpu.PrefetchScalarGridSpec(
            num_scalar_prefetch=1,
            grid=(block_count // group,),
            in_specs=[pl.BlockSpec(spectra.shape, lambda i, pr: (0, 0, 0, 0))],
            out_specs=pl.BlockSpec(
                (group, ROUNDS, 2, width, lanes), lambda i, pr: (i, 0, 0, 0, 0)
            ),
        ),
        out_shape=jax.ShapeDtypeStruct((block_count, ROUNDS, 2, width, lanes), jnp.bfloat16),
    )(pairings, spectra)

def regroup_kernel(x_ref, o_ref, *, group, width):
    lane = lax.broadcasted_iota(jnp.int32, x_ref.shape[2:], 1)
    low_lanes = lane < width

    def body(g, carry):
        for q in range(2):
            real_off = x_ref[g, 2 * q].astype(jnp.float32)
            imag_off = x_ref[g, 2 * q + 1].astype(jnp.float32)
            even = jnp.where(low_lanes, real_off, pltpu.roll(imag_off, width, 1))
            odd = jnp.where(low_lanes, pltpu.roll(real_off, width, 1), imag_off)
            rows = jnp.concatenate([even, odd], axis=0).astype(o_ref.dtype)
            o_ref[g, pl.ds(q * rows.shape[0], rows.shape[0])] = rows
        return carry

    lax.fori_loop(0, group, body, 0, unroll=8)


def regroup_stage(pooled):
    units, parts, chunks, lanes = pooled.shape
    group = 32
    kernel = functools.partial(regroup_kernel, group=group, width=lanes // 2)
    out_rows = parts * chunks
    return pl.pallas_call(
        kernel,
        grid=(units // group,),
        in_specs=[pl.BlockSpec((group, parts, chunks, lanes), lambda i: (i, 0, 0, 0))],
        out_specs=pl.BlockSpec((group, out_rows, lanes), lambda i: (i, 0, 0)),
        out_shape=jax.ShapeDtypeStruct((units, out_rows, lanes), pooled.dtype),
    )(pooled)


def unshuffle_kernel(x_ref, o_ref, *, group, width):
    for k in range(group):
        flipped = x_ref[k].T
        o_ref[k] = jnp.concatenate([flipped[:width], flipped[width:]], axis=1).astype(o_ref.dtype)


def unshuffle_stage(received):
    rows, sources, lanes = received.shape
    group = 32
    kernel = functools.partial(unshuffle_kernel, group=group, width=lanes // 2)
    return pl.pallas_call(
        kernel,
        grid=(rows // group,),
        in_specs=[pl.BlockSpec((group, sources, lanes), lambda i: (i, 0, 0))],
        out_specs=pl.BlockSpec((group, lanes // 2, 2 * sources), lambda i: (i, 0, 0)),
        out_shape=jax.ShapeDtypeStruct((rows, lanes // 2, 2 * sources), jnp.bfloat16),
    )(received)


def on_device(raw_windows, pairings):
    win_count, block_width, length = raw_windows.shape
    chan_count = lax.axis_size("chan")
    day_count = lax.axis_size("tm")
    per_piece = F // (chan_count * day_count)
    dft_table = band_table(chan_count, day_count)
    flat_raw = raw_windows.reshape(win_count * block_width, length)
    spectra = lax.dot_general(
        dft_table, flat_raw, (((1,), (1,)), ((), ())), preferred_element_type=jnp.float32
    )
    power_sum = jnp.sum(spectra * spectra, axis=0) / F
    whitened = (spectra * lax.rsqrt(power_sum + 1e-06)[None, :]).astype(jnp.bfloat16)
    layered = whitened.reshape(chan_count * day_count, 2 * per_piece, win_count * block_width)
    scale_value = 1.0 / math.sqrt(win_count * day_count)
    pooled = lax.all_to_all(layered, ("chan", "tm"), split_axis=0, concat_axis=0, tiled=True)
    lanes = per_piece * block_width
    split = pooled.reshape(chan_count * day_count, 2 * per_piece, win_count * block_width // lanes, lanes)
    by_block = regroup_stage(split).reshape(chan_count, day_count, 2 * win_count, lanes)
    tiles = pair_stage(pairings, by_block, scale_value)
    rows = ROUNDS * 2 * block_width
    tiles = tiles.reshape(chan_count, rows, 1, 2 * block_width)
    received = lax.all_to_all(tiles, "chan", split_axis=0, concat_axis=2, tiled=True)
    stacked = unshuffle_stage(received.reshape(rows, chan_count, 2 * block_width))
    return stacked.reshape(ROUNDS, 2, block_width, block_width, per_piece * chan_count)

def solution(mesh):
    return jax.shard_map(
        on_device,
        mesh=mesh,
        in_specs=(P("tm", "chan", None), P()),
        out_specs=P(None, None, "chan", None, "tm"),
        check_vma=False,
    )
```

```python
import functools
import math

import jax
import ml_dtypes
import numpy as np
import jax.numpy as jnp
from jax import lax
from jax.experimental import pallas as pl
from jax.experimental.pallas import tpu as pltpu
from jax.sharding import PartitionSpec as P

F = 512
L = 2048
ROUNDS = 2


def band_table(chan_count, day_count):
    per_piece = F // (chan_count * day_count)
    row_ids = np.arange(2 * F, dtype=np.int64)
    piece_idx = row_ids // (day_count * 2 * per_piece)
    remainder = row_ids % (day_count * 2 * per_piece)
    group_idx = remainder // (2 * per_piece)
    within = remainder % (2 * per_piece)
    imag_flag = within // per_piece
    offset_idx = within % per_piece
    freq_ids = group_idx * (chan_count * per_piece) + offset_idx * chan_count + piece_idx
    samples = np.arange(L, dtype=np.int64)
    angles = ((freq_ids[:, None] + 1) * samples[None, :] % L) * (2.0 * np.pi / L)
    taper_vals = 0.5 - 0.5 * np.cos((samples + 0.5) * (2.0 * np.pi / L))
    values = np.where(imag_flag[:, None] == 0, np.cos(angles), -np.sin(angles)) * taper_vals[None]
    return jnp.asarray(values.astype(ml_dtypes.bfloat16))

def pair_kernel(pair_ref, x_ref, o_ref, *, group, day_count, half, width, scale_value):
    step = pl.program_id(0)
    rows = 2 * 2 * half
    row_part = lax.broadcasted_iota(jnp.int32, (rows, 2 * width), 0) // (2 * half)
    lane_part = lax.broadcasted_iota(jnp.int32, (rows, 2 * width), 1) // width
    diagonal = row_part == lane_part

    def spread(part):
        stacked = jnp.concatenate([part, part], axis=0)
        return jnp.where(diagonal, stacked, jnp.zeros_like(stacked))

    def body(k, carry):
        block = step * group + k
        partners = [pair_ref[r, block] for r in range(ROUNDS)]
        accs = [jnp.zeros((width, 4 * width), jnp.float32) for _ in range(ROUNDS)]
        for day in range(day_count):
            own = x_ref[block, day]
            lhs = jnp.concatenate([own[:, :width], own[:, width:]], axis=0)
            for r in range(ROUNDS):
                other = x_ref[partners[r], day]
                rotated = jnp.concatenate([-other[half:], other[:half]], axis=0)
                rhs = jnp.concatenate([spread(other), spread(rotated)], axis=1)
                prod = lax.dot_general(
                    lhs, rhs, (((0,), (0,)), ((), ())), preferred_element_type=jnp.float32
                )
                accs[r] = accs[r] + prod.astype(jnp.bfloat16).astype(jnp.float32)
        for r in range(ROUNDS):
            scaled = (accs[r] * scale_value).astype(jnp.bfloat16)
            o_ref[k, r, 0] = scaled[:, :2 * width]
            o_ref[k, r, 1] = scaled[:, 2 * width:]
        return carry

    lax.fori_loop(0, group, body, 0, unroll=8)


def pair_stage(pairings, spectra, scale_value):
    block_count, day_count, rows, lanes = spectra.shape
    width = lanes // 2
    group = 8
    kernel = functools.partial(
        pair_kernel, group=group, day_count=day_count, half=rows // 2, width=width,
        scale_value=scale_value,
    )
    return pl.pallas_call(
        kernel,
        grid_spec=pltpu.PrefetchScalarGridSpec(
            num_scalar_prefetch=1,
            grid=(block_count // group,),
            in_specs=[pl.BlockSpec(spectra.shape, lambda i, pr: (0, 0, 0, 0))],
            out_specs=pl.BlockSpec(
                (group, ROUNDS, 2, width, lanes), lambda i, pr: (i, 0, 0, 0, 0)
            ),
        ),
        out_shape=jax.ShapeDtypeStruct((block_count, ROUNDS, 2, width, lanes), jnp.bfloat16),
    )(pairings, spectra)

def regroup_kernel(x_ref, o_ref, *, group, width):
    lane = lax.broadcasted_iota(jnp.int32, x_ref.shape[2:], 1)
    low_lanes = lane < width

    def body(g, carry):
        for q in range(2):
            real_off = x_ref[g, 2 * q].astype(jnp.float32)
            imag_off = x_ref[g, 2 * q + 1].astype(jnp.float32)
            even = jnp.where(low_lanes, real_off, pltpu.roll(imag_off, width, 1))
            odd = jnp.where(low_lanes, pltpu.roll(real_off, width, 1), imag_off)
            rows = jnp.concatenate([even, odd], axis=0).astype(o_ref.dtype)
            o_ref[g, pl.ds(q * rows.shape[0], rows.shape[0])] = rows
        return carry

    lax.fori_loop(0, group, body, 0, unroll=8)


def regroup_stage(pooled):
    units, parts, chunks, lanes = pooled.shape
    group = 32
    kernel = functools.partial(regroup_kernel, group=group, width=lanes // 2)
    out_rows = parts * chunks
    return pl.pallas_call(
        kernel,
        grid=(units // group,),
        in_specs=[pl.BlockSpec((group, parts, chunks, lanes), lambda i: (i, 0, 0, 0))],
        out_specs=pl.BlockSpec((group, out_rows, lanes), lambda i: (i, 0, 0)),
        out_shape=jax.ShapeDtypeStruct((units, out_rows, lanes), pooled.dtype),
    )(pooled)


def unshuffle_kernel(x_ref, o_ref, *, group, width):
    for k in range(group):
        flipped = x_ref[k].T
        o_ref[k] = jnp.concatenate([flipped[:width], flipped[width:]], axis=1).astype(o_ref.dtype)


def unshuffle_stage(received):
    rows, sources, lanes = received.shape
    group = 64
    kernel = functools.partial(unshuffle_kernel, group=group, width=lanes // 2)
    return pl.pallas_call(
        kernel,
        grid=(rows // group,),
        in_specs=[pl.BlockSpec((group, sources, lanes), lambda i: (i, 0, 0))],
        out_specs=pl.BlockSpec((group, lanes // 2, 2 * sources), lambda i: (i, 0, 0)),
        out_shape=jax.ShapeDtypeStruct((rows, lanes // 2, 2 * sources), jnp.bfloat16),
    )(received)


def on_device(raw_windows, pairings):
    win_count, block_width, length = raw_windows.shape
    chan_count = lax.axis_size("chan")
    day_count = lax.axis_size("tm")
    per_piece = F // (chan_count * day_count)
    dft_table = band_table(chan_count, day_count)
    flat_raw = raw_windows.reshape(win_count * block_width, length)
    spectra = lax.dot_general(
        dft_table, flat_raw, (((1,), (1,)), ((), ())), preferred_element_type=jnp.float32
    )
    power_sum = jnp.sum(spectra * spectra, axis=0) / F
    whitened = (spectra * lax.rsqrt(power_sum + 1e-06)[None, :]).astype(jnp.bfloat16)
    layered = whitened.reshape(chan_count * day_count, 2 * per_piece, win_count * block_width)
    scale_value = 1.0 / math.sqrt(win_count * day_count)
    pooled = lax.all_to_all(layered, ("chan", "tm"), split_axis=0, concat_axis=0, tiled=True)
    lanes = per_piece * block_width
    split = pooled.reshape(chan_count * day_count, 2 * per_piece, win_count * block_width // lanes, lanes)
    by_block = regroup_stage(split).reshape(chan_count, day_count, 2 * win_count, lanes)
    tiles = pair_stage(pairings, by_block, scale_value)
    rows = ROUNDS * 2 * block_width
    tiles = tiles.reshape(chan_count, rows, 1, 2 * block_width)
    received = lax.all_to_all(tiles, "chan", split_axis=0, concat_axis=2, tiled=True)
    stacked = unshuffle_stage(received.reshape(rows, chan_count, 2 * block_width))
    return stacked.reshape(ROUNDS, 2, block_width, block_width, per_piece * chan_count)

def solution(mesh):
    return jax.shard_map(
        on_device,
        mesh=mesh,
        in_specs=(P("tm", "chan", None), P()),
        out_specs=P(None, None, "chan", None, "tm"),
        check_vma=False,
    )
```

```python
import functools
import math

import jax
import ml_dtypes
import numpy as np
import jax.numpy as jnp
from jax import lax
from jax.experimental import pallas as pl
from jax.experimental.pallas import tpu as pltpu
from jax.sharding import PartitionSpec as P

F = 512
L = 2048
ROUNDS = 2


def band_table(chan_count, day_count):
    per_piece = F // (chan_count * day_count)
    row_ids = np.arange(2 * F, dtype=np.int64)
    piece_idx = row_ids // (day_count * 2 * per_piece)
    remainder = row_ids % (day_count * 2 * per_piece)
    group_idx = remainder // (2 * per_piece)
    within = remainder % (2 * per_piece)
    imag_flag = within // per_piece
    offset_idx = within % per_piece
    freq_ids = group_idx * (chan_count * per_piece) + offset_idx * chan_count + piece_idx
    samples = np.arange(L, dtype=np.int64)
    angles = ((freq_ids[:, None] + 1) * samples[None, :] % L) * (2.0 * np.pi / L)
    taper_vals = 0.5 - 0.5 * np.cos((samples + 0.5) * (2.0 * np.pi / L))
    values = np.where(imag_flag[:, None] == 0, np.cos(angles), -np.sin(angles)) * taper_vals[None]
    return jnp.asarray(values.astype(ml_dtypes.bfloat16))

def pair_kernel(pair_ref, x_ref, o_ref, *, group, day_count, half, width, scale_value):
    step = pl.program_id(0)
    rows = 2 * 2 * half
    row_part = lax.broadcasted_iota(jnp.int32, (rows, 2 * width), 0) // (2 * half)
    lane_part = lax.broadcasted_iota(jnp.int32, (rows, 2 * width), 1) // width
    diagonal = row_part == lane_part

    def spread(part):
        stacked = jnp.concatenate([part, part], axis=0)
        return jnp.where(diagonal, stacked, jnp.zeros_like(stacked))

    def body(k, carry):
        block = step * group + k
        partners = [pair_ref[r, block] for r in range(ROUNDS)]
        accs = [jnp.zeros((width, 4 * width), jnp.float32) for _ in range(ROUNDS)]
        for day in range(day_count):
            own = x_ref[block, day]
            lhs = jnp.concatenate([own[:, :width], own[:, width:]], axis=0)
            for r in range(ROUNDS):
                other = x_ref[partners[r], day]
                rotated = jnp.concatenate([-other[half:], other[:half]], axis=0)
                rhs = jnp.concatenate([spread(other), spread(rotated)], axis=1)
                prod = lax.dot_general(
                    lhs, rhs, (((0,), (0,)), ((), ())), preferred_element_type=jnp.float32
                )
                accs[r] = accs[r] + prod.astype(jnp.bfloat16).astype(jnp.float32)
        for r in range(ROUNDS):
            scaled = (accs[r] * scale_value).astype(jnp.bfloat16)
            o_ref[k, r, 0] = scaled[:, :2 * width]
            o_ref[k, r, 1] = scaled[:, 2 * width:]
        return carry

    lax.fori_loop(0, group, body, 0, unroll=8)


def pair_stage(pairings, spectra, scale_value):
    block_count, day_count, rows, lanes = spectra.shape
    width = lanes // 2
    group = 8
    kernel = functools.partial(
        pair_kernel, group=group, day_count=day_count, half=rows // 2, width=width,
        scale_value=scale_value,
    )
    return pl.pallas_call(
        kernel,
        grid_spec=pltpu.PrefetchScalarGridSpec(
            num_scalar_prefetch=1,
            grid=(block_count // group,),
            in_specs=[pl.BlockSpec(spectra.shape, lambda i, pr: (0, 0, 0, 0))],
            out_specs=pl.BlockSpec(
                (group, ROUNDS, 2, width, lanes), lambda i, pr: (i, 0, 0, 0, 0)
            ),
        ),
        out_shape=jax.ShapeDtypeStruct((block_count, ROUNDS, 2, width, lanes), jnp.bfloat16),
    )(pairings, spectra)

def regroup_kernel(x_ref, o_ref, *, group, width):
    lane = lax.broadcasted_iota(jnp.int32, x_ref.shape[2:], 1)
    low_lanes = lane < width

    def body(g, carry):
        for q in range(2):
            real_off = x_ref[g, 2 * q].astype(jnp.float32)
            imag_off = x_ref[g, 2 * q + 1].astype(jnp.float32)
            even = jnp.where(low_lanes, real_off, pltpu.roll(imag_off, width, 1))
            odd = jnp.where(low_lanes, pltpu.roll(real_off, width, 1), imag_off)
            rows = jnp.concatenate([even, odd], axis=0).astype(o_ref.dtype)
            o_ref[g, pl.ds(q * rows.shape[0], rows.shape[0])] = rows
        return carry

    lax.fori_loop(0, group, body, 0, unroll=8)


def regroup_stage(pooled):
    units, parts, chunks, lanes = pooled.shape
    group = 64
    kernel = functools.partial(regroup_kernel, group=group, width=lanes // 2)
    out_rows = parts * chunks
    return pl.pallas_call(
        kernel,
        grid=(units // group,),
        in_specs=[pl.BlockSpec((group, parts, chunks, lanes), lambda i: (i, 0, 0, 0))],
        out_specs=pl.BlockSpec((group, out_rows, lanes), lambda i: (i, 0, 0)),
        out_shape=jax.ShapeDtypeStruct((units, out_rows, lanes), pooled.dtype),
    )(pooled)


def unshuffle_kernel(x_ref, o_ref, *, group, width):
    for k in range(group):
        flipped = x_ref[k].T
        o_ref[k] = jnp.concatenate([flipped[:width], flipped[width:]], axis=1).astype(o_ref.dtype)


def unshuffle_stage(received):
    rows, sources, lanes = received.shape
    group = 64
    kernel = functools.partial(unshuffle_kernel, group=group, width=lanes // 2)
    return pl.pallas_call(
        kernel,
        grid=(rows // group,),
        in_specs=[pl.BlockSpec((group, sources, lanes), lambda i: (i, 0, 0))],
        out_specs=pl.BlockSpec((group, lanes // 2, 2 * sources), lambda i: (i, 0, 0)),
        out_shape=jax.ShapeDtypeStruct((rows, lanes // 2, 2 * sources), jnp.bfloat16),
    )(received)


def on_device(raw_windows, pairings):
    win_count, block_width, length = raw_windows.shape
    chan_count = lax.axis_size("chan")
    day_count = lax.axis_size("tm")
    per_piece = F // (chan_count * day_count)
    dft_table = band_table(chan_count, day_count)
    flat_raw = raw_windows.reshape(win_count * block_width, length)
    spectra = lax.dot_general(
        dft_table, flat_raw, (((1,), (1,)), ((), ())), preferred_element_type=jnp.float32
    )
    power_sum = jnp.sum(spectra * spectra, axis=0) / F
    whitened = (spectra * lax.rsqrt(power_sum + 1e-06)[None, :]).astype(jnp.bfloat16)
    layered = whitened.reshape(chan_count * day_count, 2 * per_piece, win_count * block_width)
    scale_value = 1.0 / math.sqrt(win_count * day_count)
    pooled = lax.all_to_all(layered, ("chan", "tm"), split_axis=0, concat_axis=0, tiled=True)
    lanes = per_piece * block_width
    split = pooled.reshape(chan_count * day_count, 2 * per_piece, win_count * block_width // lanes, lanes)
    by_block = regroup_stage(split).reshape(chan_count, day_count, 2 * win_count, lanes)
    tiles = pair_stage(pairings, by_block, scale_value)
    rows = ROUNDS * 2 * block_width
    tiles = tiles.reshape(chan_count, rows, 1, 2 * block_width)
    received = lax.all_to_all(tiles, "chan", split_axis=0, concat_axis=2, tiled=True)
    stacked = unshuffle_stage(received.reshape(rows, chan_count, 2 * block_width))
    return stacked.reshape(ROUNDS, 2, block_width, block_width, per_piece * chan_count)

def solution(mesh):
    return jax.shard_map(
        on_device,
        mesh=mesh,
        in_specs=(P("tm", "chan", None), P()),
        out_specs=P(None, None, "chan", None, "tm"),
        check_vma=False,
    )
```

```python
import functools
import math

import jax
import ml_dtypes
import numpy as np
import jax.numpy as jnp
from jax import lax
from jax.experimental import pallas as pl
from jax.experimental.pallas import tpu as pltpu
from jax.sharding import PartitionSpec as P

F = 512
L = 2048
ROUNDS = 2


def band_table(chan_count, day_count):
    per_piece = F // (chan_count * day_count)
    row_ids = np.arange(2 * F, dtype=np.int64)
    piece_idx = row_ids // (day_count * 2 * per_piece)
    remainder = row_ids % (day_count * 2 * per_piece)
    group_idx = remainder // (2 * per_piece)
    within = remainder % (2 * per_piece)
    imag_flag = within // per_piece
    offset_idx = within % per_piece
    freq_ids = group_idx * (chan_count * per_piece) + offset_idx * chan_count + piece_idx
    samples = np.arange(L, dtype=np.int64)
    angles = ((freq_ids[:, None] + 1) * samples[None, :] % L) * (2.0 * np.pi / L)
    taper_vals = 0.5 - 0.5 * np.cos((samples + 0.5) * (2.0 * np.pi / L))
    values = np.where(imag_flag[:, None] == 0, np.cos(angles), -np.sin(angles)) * taper_vals[None]
    return jnp.asarray(values.astype(ml_dtypes.bfloat16))

def pair_kernel(pair_ref, x_ref, o_ref, *, group, day_count, half, width, scale_value):
    step = pl.program_id(0)
    rows = 2 * 2 * half
    row_part = lax.broadcasted_iota(jnp.int32, (rows, 2 * width), 0) // (2 * half)
    lane_part = lax.broadcasted_iota(jnp.int32, (rows, 2 * width), 1) // width
    diagonal = row_part == lane_part

    def spread(part):
        stacked = jnp.concatenate([part, part], axis=0)
        return jnp.where(diagonal, stacked, jnp.zeros_like(stacked))

    def body(k, carry):
        block = step * group + k
        partners = [pair_ref[r, block] for r in range(ROUNDS)]
        accs = [jnp.zeros((width, 4 * width), jnp.float32) for _ in range(ROUNDS)]
        for day in range(day_count):
            own = x_ref[block, day]
            lhs = jnp.concatenate([own[:, :width], own[:, width:]], axis=0)
            for r in range(ROUNDS):
                other = x_ref[partners[r], day]
                rotated = jnp.concatenate([-other[half:], other[:half]], axis=0)
                rhs = jnp.concatenate([spread(other), spread(rotated)], axis=1)
                prod = lax.dot_general(
                    lhs, rhs, (((0,), (0,)), ((), ())), preferred_element_type=jnp.float32
                )
                accs[r] = accs[r] + prod.astype(jnp.bfloat16).astype(jnp.float32)
        for r in range(ROUNDS):
            scaled = (accs[r] * scale_value).astype(jnp.bfloat16)
            o_ref[k, r, 0] = scaled[:, :2 * width]
            o_ref[k, r, 1] = scaled[:, 2 * width:]
        return carry

    lax.fori_loop(0, group, body, 0, unroll=8)


def pair_stage(pairings, spectra, scale_value):
    block_count, day_count, rows, lanes = spectra.shape
    width = lanes // 2
    group = 16
    kernel = functools.partial(
        pair_kernel, group=group, day_count=day_count, half=rows // 2, width=width,
        scale_value=scale_value,
    )
    return pl.pallas_call(
        kernel,
        grid_spec=pltpu.PrefetchScalarGridSpec(
            num_scalar_prefetch=1,
            grid=(block_count // group,),
            in_specs=[pl.BlockSpec(spectra.shape, lambda i, pr: (0, 0, 0, 0))],
            out_specs=pl.BlockSpec(
                (group, ROUNDS, 2, width, lanes), lambda i, pr: (i, 0, 0, 0, 0)
            ),
        ),
        out_shape=jax.ShapeDtypeStruct((block_count, ROUNDS, 2, width, lanes), jnp.bfloat16),
    )(pairings, spectra)

def regroup_kernel(x_ref, o_ref, *, group, width):
    lane = lax.broadcasted_iota(jnp.int32, x_ref.shape[2:], 1)
    low_lanes = lane < width

    def body(g, carry):
        for q in range(2):
            real_off = x_ref[g, 2 * q].astype(jnp.float32)
            imag_off = x_ref[g, 2 * q + 1].astype(jnp.float32)
            even = jnp.where(low_lanes, real_off, pltpu.roll(imag_off, width, 1))
            odd = jnp.where(low_lanes, pltpu.roll(real_off, width, 1), imag_off)
            rows = jnp.concatenate([even, odd], axis=0).astype(o_ref.dtype)
            o_ref[g, pl.ds(q * rows.shape[0], rows.shape[0])] = rows
        return carry

    lax.fori_loop(0, group, body, 0, unroll=8)


def regroup_stage(pooled):
    units, parts, chunks, lanes = pooled.shape
    group = 64
    kernel = functools.partial(regroup_kernel, group=group, width=lanes // 2)
    out_rows = parts * chunks
    return pl.pallas_call(
        kernel,
        grid=(units // group,),
        in_specs=[pl.BlockSpec((group, parts, chunks, lanes), lambda i: (i, 0, 0, 0))],
        out_specs=pl.BlockSpec((group, out_rows, lanes), lambda i: (i, 0, 0)),
        out_shape=jax.ShapeDtypeStruct((units, out_rows, lanes), pooled.dtype),
    )(pooled)


def unshuffle_kernel(x_ref, o_ref, *, group, width):
    for k in range(group):
        flipped = x_ref[k].T
        o_ref[k] = jnp.concatenate([flipped[:width], flipped[width:]], axis=1).astype(o_ref.dtype)


def unshuffle_stage(received):
    rows, sources, lanes = received.shape
    group = 64
    kernel = functools.partial(unshuffle_kernel, group=group, width=lanes // 2)
    return pl.pallas_call(
        kernel,
        grid=(rows // group,),
        in_specs=[pl.BlockSpec((group, sources, lanes), lambda i: (i, 0, 0))],
        out_specs=pl.BlockSpec((group, lanes // 2, 2 * sources), lambda i: (i, 0, 0)),
        out_shape=jax.ShapeDtypeStruct((rows, lanes // 2, 2 * sources), jnp.bfloat16),
    )(received)


def on_device(raw_windows, pairings):
    win_count, block_width, length = raw_windows.shape
    chan_count = lax.axis_size("chan")
    day_count = lax.axis_size("tm")
    per_piece = F // (chan_count * day_count)
    dft_table = band_table(chan_count, day_count)
    flat_raw = raw_windows.reshape(win_count * block_width, length)
    spectra = lax.dot_general(
        dft_table, flat_raw, (((1,), (1,)), ((), ())), preferred_element_type=jnp.float32
    )
    power_sum = jnp.sum(spectra * spectra, axis=0) / F
    whitened = (spectra * lax.rsqrt(power_sum + 1e-06)[None, :]).astype(jnp.bfloat16)
    layered = whitened.reshape(chan_count * day_count, 2 * per_piece, win_count * block_width)
    scale_value = 1.0 / math.sqrt(win_count * day_count)
    pooled = lax.all_to_all(layered, ("chan", "tm"), split_axis=0, concat_axis=0, tiled=True)
    lanes = per_piece * block_width
    split = pooled.reshape(chan_count * day_count, 2 * per_piece, win_count * block_width // lanes, lanes)
    by_block = regroup_stage(split).reshape(chan_count, day_count, 2 * win_count, lanes)
    tiles = pair_stage(pairings, by_block, scale_value)
    rows = ROUNDS * 2 * block_width
    tiles = tiles.reshape(chan_count, rows, 1, 2 * block_width)
    received = lax.all_to_all(tiles, "chan", split_axis=0, concat_axis=2, tiled=True)
    stacked = unshuffle_stage(received.reshape(rows, chan_count, 2 * block_width))
    return stacked.reshape(ROUNDS, 2, block_width, block_width, per_piece * chan_count)

def solution(mesh):
    return jax.shard_map(
        on_device,
        mesh=mesh,
        in_specs=(P("tm", "chan", None), P()),
        out_specs=P(None, None, "chan", None, "tm"),
        check_vma=False,
    )
```

```python
import functools
import math

import jax
import ml_dtypes
import numpy as np
import jax.numpy as jnp
from jax import lax
from jax.experimental import pallas as pl
from jax.experimental.pallas import tpu as pltpu
from jax.sharding import PartitionSpec as P

F = 512
L = 2048
ROUNDS = 2


def band_table(chan_count, day_count):
    per_piece = F // (chan_count * day_count)
    row_ids = np.arange(2 * F, dtype=np.int64)
    piece_idx = row_ids // (day_count * 2 * per_piece)
    remainder = row_ids % (day_count * 2 * per_piece)
    group_idx = remainder // (2 * per_piece)
    within = remainder % (2 * per_piece)
    imag_flag = within // per_piece
    offset_idx = within % per_piece
    freq_ids = group_idx * (chan_count * per_piece) + offset_idx * chan_count + piece_idx
    samples = np.arange(L, dtype=np.int64)
    angles = ((freq_ids[:, None] + 1) * samples[None, :] % L) * (2.0 * np.pi / L)
    taper_vals = 0.5 - 0.5 * np.cos((samples + 0.5) * (2.0 * np.pi / L))
    values = np.where(imag_flag[:, None] == 0, np.cos(angles), -np.sin(angles)) * taper_vals[None]
    return jnp.asarray(values.astype(ml_dtypes.bfloat16))

def pair_kernel(pair_ref, x_ref, o_ref, *, group, day_count, half, width, scale_value):
    step = pl.program_id(0)
    rows = 2 * 2 * half
    row_part = lax.broadcasted_iota(jnp.int32, (rows, 2 * width), 0) // (2 * half)
    lane_part = lax.broadcasted_iota(jnp.int32, (rows, 2 * width), 1) // width
    diagonal = row_part == lane_part

    def spread(part):
        stacked = jnp.concatenate([part, part], axis=0)
        return jnp.where(diagonal, stacked, jnp.zeros_like(stacked))

    def body(k, carry):
        block = step * group + k
        partners = [pair_ref[r, block] for r in range(ROUNDS)]
        accs = [jnp.zeros((width, 4 * width), jnp.float32) for _ in range(ROUNDS)]
        for day in range(day_count):
            own = x_ref[block, day]
            lhs = jnp.concatenate([own[:, :width], own[:, width:]], axis=0)
            for r in range(ROUNDS):
                other = x_ref[partners[r], day]
                rotated = jnp.concatenate([-other[half:], other[:half]], axis=0)
                rhs = jnp.concatenate([spread(other), spread(rotated)], axis=1)
                prod = lax.dot_general(
                    lhs, rhs, (((0,), (0,)), ((), ())), preferred_element_type=jnp.float32
                )
                accs[r] = accs[r] + prod.astype(jnp.bfloat16).astype(jnp.float32)
        for r in range(ROUNDS):
            scaled = (accs[r] * scale_value).astype(jnp.bfloat16)
            o_ref[k, r, 0] = scaled[:, :2 * width]
            o_ref[k, r, 1] = scaled[:, 2 * width:]
        return carry

    lax.fori_loop(0, group, body, 0, unroll=8)


def pair_stage(pairings, spectra, scale_value):
    block_count, day_count, rows, lanes = spectra.shape
    width = lanes // 2
    group = 8
    kernel = functools.partial(
        pair_kernel, group=group, day_count=day_count, half=rows // 2, width=width,
        scale_value=scale_value,
    )
    return pl.pallas_call(
        kernel,
        grid_spec=pltpu.PrefetchScalarGridSpec(
            num_scalar_prefetch=1,
            grid=(block_count // group,),
            in_specs=[pl.BlockSpec(spectra.shape, lambda i, pr: (0, 0, 0, 0))],
            out_specs=pl.BlockSpec(
                (group, ROUNDS, 2, width, lanes), lambda i, pr: (i, 0, 0, 0, 0)
            ),
        ),
        out_shape=jax.ShapeDtypeStruct((block_count, ROUNDS, 2, width, lanes), jnp.bfloat16),
    )(pairings, spectra)

def regroup_kernel(x_ref, o_ref, *, group, width):
    lane = lax.broadcasted_iota(jnp.int32, x_ref.shape[2:], 1)
    low_lanes = lane < width

    def body(g, carry):
        for q in range(2):
            real_off = x_ref[g, 2 * q].astype(jnp.float32)
            imag_off = x_ref[g, 2 * q + 1].astype(jnp.float32)
            even = jnp.where(low_lanes, real_off, pltpu.roll(imag_off, width, 1))
            odd = jnp.where(low_lanes, pltpu.roll(real_off, width, 1), imag_off)
            rows = jnp.concatenate([even, odd], axis=0).astype(o_ref.dtype)
            o_ref[g, pl.ds(q * rows.shape[0], rows.shape[0])] = rows
        return carry

    lax.fori_loop(0, group, body, 0, unroll=16)


def regroup_stage(pooled):
    units, parts, chunks, lanes = pooled.shape
    group = 64
    kernel = functools.partial(regroup_kernel, group=group, width=lanes // 2)
    out_rows = parts * chunks
    return pl.pallas_call(
        kernel,
        grid=(units // group,),
        in_specs=[pl.BlockSpec((group, parts, chunks, lanes), lambda i: (i, 0, 0, 0))],
        out_specs=pl.BlockSpec((group, out_rows, lanes), lambda i: (i, 0, 0)),
        out_shape=jax.ShapeDtypeStruct((units, out_rows, lanes), pooled.dtype),
    )(pooled)


def unshuffle_kernel(x_ref, o_ref, *, group, width):
    for k in range(group):
        flipped = x_ref[k].T
        o_ref[k] = jnp.concatenate([flipped[:width], flipped[width:]], axis=1).astype(o_ref.dtype)


def unshuffle_stage(received):
    rows, sources, lanes = received.shape
    group = 64
    kernel = functools.partial(unshuffle_kernel, group=group, width=lanes // 2)
    return pl.pallas_call(
        kernel,
        grid=(rows // group,),
        in_specs=[pl.BlockSpec((group, sources, lanes), lambda i: (i, 0, 0))],
        out_specs=pl.BlockSpec((group, lanes // 2, 2 * sources), lambda i: (i, 0, 0)),
        out_shape=jax.ShapeDtypeStruct((rows, lanes // 2, 2 * sources), jnp.bfloat16),
    )(received)


def on_device(raw_windows, pairings):
    win_count, block_width, length = raw_windows.shape
    chan_count = lax.axis_size("chan")
    day_count = lax.axis_size("tm")
    per_piece = F // (chan_count * day_count)
    dft_table = band_table(chan_count, day_count)
    flat_raw = raw_windows.reshape(win_count * block_width, length)
    spectra = lax.dot_general(
        dft_table, flat_raw, (((1,), (1,)), ((), ())), preferred_element_type=jnp.float32
    )
    power_sum = jnp.sum(spectra * spectra, axis=0) / F
    whitened = (spectra * lax.rsqrt(power_sum + 1e-06)[None, :]).astype(jnp.bfloat16)
    layered = whitened.reshape(chan_count * day_count, 2 * per_piece, win_count * block_width)
    scale_value = 1.0 / math.sqrt(win_count * day_count)
    pooled = lax.all_to_all(layered, ("chan", "tm"), split_axis=0, concat_axis=0, tiled=True)
    lanes = per_piece * block_width
    split = pooled.reshape(chan_count * day_count, 2 * per_piece, win_count * block_width // lanes, lanes)
    by_block = regroup_stage(split).reshape(chan_count, day_count, 2 * win_count, lanes)
    tiles = pair_stage(pairings, by_block, scale_value)
    rows = ROUNDS * 2 * block_width
    tiles = tiles.reshape(chan_count, rows, 1, 2 * block_width)
    received = lax.all_to_all(tiles, "chan", split_axis=0, concat_axis=2, tiled=True)
    stacked = unshuffle_stage(received.reshape(rows, chan_count, 2 * block_width))
    return stacked.reshape(ROUNDS, 2, block_width, block_width, per_piece * chan_count)

def solution(mesh):
    return jax.shard_map(
        on_device,
        mesh=mesh,
        in_specs=(P("tm", "chan", None), P()),
        out_specs=P(None, None, "chan", None, "tm"),
        check_vma=False,
    )
```
